512 devices in a mesh: gx: 64 (over z, x, core), vert: 8 (over y).
Axes of the slice: x: 4, y: 8, z: 8, core: 2. Of those that a mesh axis runs over, the one named last changes fastest.
Arguments:
- position_factor: float32 [64, 8, 16, 256], P('gx'), may hold values from -6 to 6
- coefficients: float32 [256, 256], replicated, may hold values from -1 to 3
- velocity_factor: float32 [8, 64, 128, 256], P('vert', 'gx'), may hold values from -6 to 6
- gravity: float32 [3, 64, 8, 16], P(None, 'gx'), may hold values from -6 to 6
Outputs:
- new_position: float32 [64, 8, 16, 256], P('gx')
- new_velocity: float32 [8, 64, 128, 256], P('vert', 'gx')
The draws below stay inside these ranges and needn't reach their ends.
All inputs are finite; a program needn't handle non-finite values.
Results may differ from the reference program's by a relative error of at most 0.0001.
Values sent between devices are 32-bit elements; how exact they have to be, the bound alone decides.
No kernel may reach another device: no remote copies, remote signals or barrier semaphores. Data moves between devices by JAX's collectives and lax.ppermute only.
A program may use at most 64 MiB of HBM per device.

```python
import math
import jax
import jax.numpy as jnp
from jax import lax

RANK = 256
NY = 8
NZ = 16
VC = 128
NS_STEPS = 8
NX = 64
VA = 8
VB = 64
POS_CELLS = 8192
VEL_CELLS = 65536


def draw_coefficients(key, part):
    diag_key = jax.random.fold_in(key, 11)
    rest_key = jax.random.fold_in(key, 12)
    diagonal = jax.random.uniform(diag_key, (RANK,), jnp.float32, 1.5, 2.5)
    spread = jax.random.normal(rest_key, (RANK, RANK), jnp.float32) * 0.4
    return spread / math.sqrt(RANK) + jnp.diag(diagonal)


def steps_of(own_key, shape, cuts, smallest, top_value):
    def one(dim, parts):
        draws = jax.random.uniform(jax.random.fold_in(jax.random.fold_in(own_key, 6), dim), (parts,), jnp.float32, smallest / len(cuts), top_value / len(cuts))
        return jnp.repeat(jnp.exp(draws), shape[dim] // parts).reshape((-1,) + (1,) * (len(shape) - dim - 1))

    factor_of = one(*cuts[0])
    for cut in cuts[1:]:
        factor_of = factor_of * one(*cut)
    return factor_of


def centred(stream_key, shape, width, bound, split=(), kind=jnp.bfloat16):
    entries = jax.random.normal(stream_key, shape, jnp.float32) * width
    if len(split) > 0:
        entries = steps_of(stream_key, shape, split, -0.22, 0.18) * entries
    return jnp.clip(entries, min=-bound, max=bound).astype(kind)


def setup_inputs(seed: int = 0) -> dict:
    streams_of = jax.random.split(jax.random.key(seed), 5)
    return {
        "position_factor": centred(streams_of[0], (NX, NY, NZ, RANK), 1.0, 6.0, ((0, 64),), jnp.float32),
        "coefficients": draw_coefficients(jax.random.fold_in(streams_of[4], 71), 0),
        "velocity_factor": centred(streams_of[2], (VA, VB, VC, RANK), 1.0, 6.0, ((0, 8), (1, 64)), jnp.float32),
        "gravity": centred(streams_of[3], (3, NX, NY, NZ), 1.0, 6.0, ((1, 64),), jnp.float32),
    }


HIGHEST = lax.Precision.HIGHEST
TIME_STEP = 0.25
NORM_EPSILON = 1e-06

def central(values, which_dim):
    padding = [(0, 0)] * values.ndim
    padding[which_dim] = (1, 1)
    padded = jnp.pad(values, padding)
    extent = values.shape[which_dim]
    return 0.5 * (lax.slice_in_dim(padded, 2, extent + 2, axis=which_dim) - lax.slice_in_dim(padded, 0, extent, axis=which_dim))

def gradient(values):
    return jnp.stack([central(values, 0), central(values, 1), central(values, 2)])

def coordinate(indices, cell_total):
    return (2.0 * indices.astype(jnp.float32) + 1.0 - cell_total) / cell_total

def velocity_grid(offset, slab_cells, first_count, second_offset, second_cells, second_count, third_count):
    grid_shape = (slab_cells, second_cells, third_count)
    first_axis = coordinate(offset + jnp.arange(slab_cells, dtype=jnp.int32), first_count)
    second_axis = coordinate(second_offset + jnp.arange(second_cells, dtype=jnp.int32), second_count)
    third_axis = coordinate(jnp.arange(third_count, dtype=jnp.int32), third_count)
    return jnp.stack([jnp.broadcast_to(first_axis[:, None, None], grid_shape), jnp.broadcast_to(second_axis[None, :, None], grid_shape), jnp.broadcast_to(third_axis[None, None, :], grid_shape)])

def moments(factor, others, cells_count):
    return jnp.einsum('xyzr,dxyzs->drs', factor, others, precision=HIGHEST) / cells_count

def apply_pair(first_terms, first_mats, second_terms, second_mats):
    return -(jnp.einsum('dxyzs,drs->xyzr', first_terms, first_mats, precision=HIGHEST) + jnp.einsum('dxyzs,drs->xyzr', second_terms, second_mats, precision=HIGHEST))

def newton_schulz(gram_matrix):
    frob_norm = jnp.sqrt(jnp.sum(gram_matrix * gram_matrix) + NORM_EPSILON)
    identity = jnp.eye(gram_matrix.shape[0], dtype=jnp.float32)
    root_part = gram_matrix / frob_norm
    inv_root = identity
    for sweep_index in range(NS_STEPS):
        middle = 1.5 * identity - 0.5 * jnp.dot(inv_root, root_part, precision=HIGHEST, preferred_element_type=jnp.float32)
        root_part = jnp.dot(root_part, middle, precision=HIGHEST, preferred_element_type=jnp.float32)
        inv_root = jnp.dot(middle, inv_root, precision=HIGHEST, preferred_element_type=jnp.float32)
    scale_root = jnp.sqrt(frob_norm)
    return (inv_root / scale_root, root_part * scale_root)

def sandwich(left_mats, core_matrix, right_mats):
    return jnp.einsum('dij,jk,dlk->il', left_mats, core_matrix, right_mats, precision=HIGHEST)

def reference(position_factor, coefficients, velocity_factor, gravity):
    velocity = velocity_grid(0, VA, VA, 0, VB, VB, VC)
    vel_first = moments(velocity_factor, velocity[..., None] * velocity_factor[None], VEL_CELLS)
    vel_second = moments(velocity_factor, gradient(velocity_factor), VEL_CELLS)

    def position_rate(values):
        return apply_pair(gradient(values), vel_first, gravity[..., None] * values[None], vel_second)
    initial = jnp.einsum('xyzs,sr->xyzr', position_factor, coefficients, precision=HIGHEST)
    section_one = initial + TIME_STEP * position_rate(initial)
    section_two = 0.75 * initial + 0.25 * (section_one + TIME_STEP * position_rate(section_one))
    final_section = 1.0 / 3.0 * initial + 2.0 / 3.0 * (section_two + TIME_STEP * position_rate(section_two))
    gram_matrix = jnp.einsum('xyzr,xyzs->rs', final_section, final_section, precision=HIGHEST) / POS_CELLS
    inv_root, root_part = newton_schulz(gram_matrix)
    new_position = jnp.einsum('xyzs,sr->xyzr', final_section, inv_root, precision=HIGHEST)
    pos_first = moments(new_position, gradient(new_position), POS_CELLS)
    pos_second = moments(new_position, gravity[..., None] * new_position[None], POS_CELLS)
    coupled_core = root_part + TIME_STEP * (sandwich(pos_first, root_part, vel_first) + sandwich(pos_second, root_part, vel_second))

    def velocity_rate(values):
        return apply_pair(velocity[..., None] * values[None], pos_first, gradient(values), pos_second)
    vel_initial = jnp.einsum('abcs,rs->abcr', velocity_factor, coupled_core, precision=HIGHEST)
    vel_section = vel_initial + TIME_STEP * velocity_rate(vel_initial)
    new_velocity = 0.5 * vel_initial + 0.5 * (vel_section + TIME_STEP * velocity_rate(vel_section))
    return (new_position, new_velocity)
```

```python
import jax
import jax.numpy as jnp
from jax import lax
from jax.sharding import Mesh
from jax.sharding import PartitionSpec as P

NS_STEPS = 8
GX = ("gx_0", "gx_1", "gx_2")


HIGHEST = lax.Precision.HIGHEST
TIME_STEP = 0.25
NORM_EPSILON = 1e-06


def padded_2(block, sides, width):
    for axis, dim in sides:
        count = lax.axis_size(axis)
        forward = [(i, i + 1) for i in range(count - 1)]
        backward = [(target, source) for source, target in forward]
        low = lax.ppermute(
            lax.slice_in_dim(block, block.shape[dim] - width, None, axis=dim), axis, forward
        )
        high = lax.ppermute(lax.slice_in_dim(block, 0, width, axis=dim), axis, backward)
        block = jnp.concatenate([low, block, high], axis=dim)
    return block


def extended(value, sides, width):
    edges = {}
    for axis, dim in sides:
        devices, length = (lax.axis_size(axis), value.shape[dim])
        up = [(i, (i + 1) % devices) for i in range(devices - 1)]
        last = lax.slice_in_dim(value, length - width, length, axis=dim)
        first = lax.slice_in_dim(value, 0, width, axis=dim)
        edges[dim] = (
            lax.ppermute(last, axis, up),
            lax.ppermute(first, axis, [(b, a) for a, b in up]),
        )
    done = []
    for _, dim in sides:
        low, high = edges[dim]
        around = [(width, width) if d in done else (0, 0) for d in range(value.ndim)]
        value = jnp.concatenate([jnp.pad(low, around), value, jnp.pad(high, around)], axis=dim)
        done.append(dim)
    return value


def from_behind(block, axis, distance):
    devices = range(lax.axis_size(axis))
    route = [(i - distance, i) for i in devices if i - distance in devices]
    return lax.ppermute(block, axis, route)


def filled_up(lines, devices):
    spare = -len(lines) % devices
    return jnp.pad(lines, [(0, spare)] + [(0, 0)] * (lines.ndim - 1))


def from_everyone(value, axis):
    devices = lax.axis_size(axis)
    return lax.all_to_all(
        jnp.broadcast_to(value[None], (devices, *value.shape)), axis, 0, 0, tiled=True
    )


def laid_out(pieces, dim):
    dims = list(pieces.shape[1:])
    dims[dim] *= pieces.shape[0]
    return jnp.moveaxis(pieces, 0, dim).reshape(dims)


def whole_of(value, axes, dim):
    far, near = axes
    pieces = from_everyone(from_everyone(value, far), near)
    return laid_out(pieces.swapaxes(0, 1).reshape(-1, *value.shape), dim)


def split_up(value, dim, devices):
    dims = value.shape
    pieces = value.reshape(*dims[:dim], devices, dims[dim] // devices, *dims[dim + 1 :])
    return jnp.moveaxis(pieces, dim, 0)


def sum_at_owner(value, axis, dim):
    devices = lax.axis_size(axis)
    pieces = lax.all_to_all(split_up(value, dim, devices), axis, 0, 0, tiled=True)
    return jnp.sum(pieces, axis=0)


def sum_in_two_steps(value, axes, dim):
    far, near = axes
    own = sum_at_owner(split_up(value, dim, lax.axis_size(far)), near, dim + 1)
    return jnp.sum(lax.all_to_all(own, far, 0, 0, tiled=True), axis=0)


def total_of(value, axes):
    lines = value.reshape(-1, value.shape[-1])
    padded = filled_up(lines, lax.axis_size(axes[0]) * lax.axis_size(axes[1]))
    whole = whole_of(sum_in_two_steps(padded, axes, 0), axes, 0)
    return lax.slice_in_dim(whole, 0, len(lines)).reshape(value.shape)


def total_of_2(value, axes):
    own = sum_in_two_steps(
        filled_up(value, lax.axis_size(axes[0]) * lax.axis_size(axes[1])), axes, 0
    )
    whole = whole_of(own, axes, 0)
    return whole[: len(value)].reshape(value.shape)


def in_one(arrays, axis):
    flat, at, done = (jnp.concatenate([a.reshape(-1) for a in arrays]), 0, [])
    running = total_of_2(flat, axis)
    for a in arrays:
        done.append(running[at : at + a.size].reshape(a.shape))
        at += a.size
    return tuple(done)


def split_parts(packed):
    flipped = jnp.swapaxes(packed, 1, 2)
    return jnp.stack([0.5 * (packed + flipped), 0.5 * (packed - flipped)])


def central(values, which_dim):
    padding = [(0, 0)] * values.ndim
    padding[which_dim] = (1, 1)
    padded = jnp.pad(values, padding)
    extent = values.shape[which_dim]
    return 0.5 * (
        lax.slice_in_dim(padded, 2, extent + 2, axis=which_dim)
        - lax.slice_in_dim(padded, 0, extent, axis=which_dim)
    )


def position_slopes(values):
    padded = padded_2(values, ((GX, 0),), 1)
    along_first = 0.5 * (padded[2:] - padded[:-2])
    return jnp.stack([along_first, central(values, 1), central(values, 2)])


def velocity_slopes(values):
    padded = extended(values, ((GX, 1), ("vert", 0)), 1)
    along_first = 0.5 * (padded[2:, 1:-1] - padded[:-2, 1:-1])
    along_second = 0.5 * (padded[1:-1, 2:] - padded[1:-1, :-2])
    return jnp.stack([along_first, along_second, central(values, 2)])


def coordinate(indices, cell_total):
    return (2.0 * indices.astype(jnp.float32) + 1.0 - cell_total) / cell_total


def velocity_grid(
    offset, slab_cells, first_count, second_offset, second_cells, second_count, third_count
):
    grid_shape = (slab_cells, second_cells, third_count)
    first_axis = coordinate(offset + jnp.arange(slab_cells, dtype=jnp.int32), first_count)
    second_axis = coordinate(
        second_offset + jnp.arange(second_cells, dtype=jnp.int32), second_count
    )
    third_axis = coordinate(jnp.arange(third_count, dtype=jnp.int32), third_count)
    return jnp.stack(
        [
            jnp.broadcast_to(first_axis[:, None, None], grid_shape),
            jnp.broadcast_to(second_axis[None, :, None], grid_shape),
            third_axis[None, None, :],
        ]
    )


def moments(factor, others, cells_count):
    return jnp.einsum("xyzr,dxyzs->drs", factor, others, precision=HIGHEST) / cells_count


def apply_pair(first_terms, first_mats, second_terms, second_mats):
    return -(
        jnp.einsum("dxyzs,drs->xyzr", first_terms, first_mats, precision=HIGHEST)
        + jnp.einsum("dxyzs,drs->xyzr", second_terms, second_mats, precision=HIGHEST)
    )


def newton_schulz(gram_matrix):
    frob_norm = jnp.sqrt(jnp.sum(gram_matrix * gram_matrix) + NORM_EPSILON)
    identity = jnp.eye(gram_matrix.shape[0], dtype=jnp.float32)
    root_part = gram_matrix / frob_norm
    inv_root = identity
    for sweep_index in range(NS_STEPS):
        middle = 1.5 * identity - 0.5 * jnp.dot(
            inv_root, root_part, precision=HIGHEST, preferred_element_type=jnp.float32
        )
        root_part = jnp.dot(
            root_part, middle, precision=HIGHEST, preferred_element_type=jnp.float32
        )
        inv_root = jnp.dot(middle, inv_root, precision=HIGHEST, preferred_element_type=jnp.float32)
    scale_root = jnp.sqrt(frob_norm)
    return (inv_root / scale_root, root_part * scale_root)


def sandwich(left_mats, core_matrix, right_mats):
    return jnp.einsum("dij,jk,dlk->il", left_mats, core_matrix, right_mats, precision=HIGHEST)


def per_device(position_factor, coefficients, velocity_factor, gravity):
    slab_vel = velocity_factor.shape[0]
    column_vel = velocity_factor.shape[1]
    first_count = slab_vel * lax.axis_size("vert")
    second_count = column_vel * lax.axis_size(GX)
    pos_cells = (
        position_factor.shape[0]
        * lax.axis_size(GX)
        * position_factor.shape[1]
        * position_factor.shape[2]
    )
    vel_cells = first_count * second_count * velocity_factor.shape[2]
    offset = lax.axis_index("vert") * slab_vel
    second_offset = lax.axis_index(GX) * column_vel
    velocity = velocity_grid(
        offset,
        slab_vel,
        first_count,
        second_offset,
        column_vel,
        second_count,
        velocity_factor.shape[2],
    )
    vel_first = moments(velocity_factor, velocity[..., None] * velocity_factor[None], vel_cells)
    next_plane = from_behind(velocity_factor, "vert", -1)
    next_column = from_behind(velocity_factor, GX, -1)
    following = jnp.concatenate([velocity_factor[1:], next_plane], axis=0)
    beside = jnp.concatenate([velocity_factor[:, 1:], next_column], axis=1)
    pair_sums = jnp.stack(
        [
            jnp.einsum("xyzr,xyzs->rs", velocity_factor, following, precision=HIGHEST),
            jnp.einsum("xyzr,xyzs->rs", velocity_factor, beside, precision=HIGHEST),
            jnp.einsum(
                "xyzr,xyzs->rs",
                velocity_factor[:, :, :-1],
                velocity_factor[:, :, 1:],
                precision=HIGHEST,
            ),
        ]
    )
    vel_second = 0.5 * (pair_sums - jnp.swapaxes(pair_sums, 1, 2)) / vel_cells
    vel_mats = split_parts(lax.psum(vel_first + vel_second, (*GX, "vert")))

    def position_rate(values):
        return apply_pair(
            position_slopes(values), vel_mats[0], gravity[..., None] * values[None], vel_mats[1]
        )

    initial = jnp.einsum("xyzs,sr->xyzr", position_factor, coefficients, precision=HIGHEST)
    section_one = initial + TIME_STEP * position_rate(initial)
    section_two = 0.75 * initial + 0.25 * (section_one + TIME_STEP * position_rate(section_one))
    final_section = 1.0 / 3.0 * initial + 2.0 / 3.0 * (
        section_two + TIME_STEP * position_rate(section_two)
    )
    gram_part = (
        jnp.einsum("xyzr,xyzs->rs", final_section, final_section, precision=HIGHEST) / pos_cells
    )
    raw_terms = jnp.stack(
        [
            moments(final_section, position_slopes(final_section), pos_cells),
            moments(final_section, gravity[..., None] * final_section[None], pos_cells),
        ]
    )
    packed = lax.psum(
        jnp.concatenate([gram_part[None], raw_terms[0] + raw_terms[1]]), GX
    )
    gram_matrix = 0.5 * (packed[0] + packed[0].T)
    second_raw, first_raw = split_parts(packed[1:])
    summed_terms = jnp.stack([first_raw, second_raw])
    inv_root, root_part = newton_schulz(gram_matrix)
    new_position = jnp.einsum("xyzs,sr->xyzr", final_section, inv_root, precision=HIGHEST)
    pos_mats = jnp.einsum("ir,ndij,js->ndrs", inv_root, summed_terms, inv_root, precision=HIGHEST)
    coupled_core = root_part + TIME_STEP * (
        sandwich(pos_mats[0], root_part, vel_mats[0])
        + sandwich(pos_mats[1], root_part, vel_mats[1])
    )

    def velocity_rate(values):
        return apply_pair(
            velocity[..., None] * values[None], pos_mats[0], velocity_slopes(values), pos_mats[1]
        )

    vel_initial = jnp.einsum("abcs,rs->abcr", velocity_factor, coupled_core, precision=HIGHEST)
    vel_section = vel_initial + TIME_STEP * velocity_rate(vel_initial)
    new_velocity = 0.5 * vel_initial + 0.5 * (vel_section + TIME_STEP * velocity_rate(vel_section))
    return (new_position, new_velocity)


def solution(mesh):
    finer = Mesh(
        mesh.devices.reshape(8, 4, 2, mesh.shape["vert"]), ("gx_0", "gx_1", "gx_2", "vert")
    )
    in_specs = (P(GX, None, None, None), P(), P("vert", GX, None, None), P(None, GX, None, None))
    out_specs = (P(GX, None, None, None), P("vert", GX, None, None))
    return jax.shard_map(
        per_device, mesh=finer, in_specs=in_specs, out_specs=out_specs, check_vma=False
    )
```

```python
import jax
import jax.numpy as jnp
from jax import lax
from jax.sharding import Mesh
from jax.sharding import PartitionSpec as P

NS_STEPS = 8
GX = ("gx_0", "gx_1", "gx_2")


HIGHEST = lax.Precision.HIGHEST
TIME_STEP = 0.25
NORM_EPSILON = 1e-06


def padded_2(block, sides, width):
    for axis, dim in sides:
        count = lax.axis_size(axis)
        forward = [(i, i + 1) for i in range(count - 1)]
        backward = [(target, source) for source, target in forward]
        low = lax.ppermute(
            lax.slice_in_dim(block, block.shape[dim] - width, None, axis=dim), axis, forward
        )
        high = lax.ppermute(lax.slice_in_dim(block, 0, width, axis=dim), axis, backward)
        block = jnp.concatenate([low, block, high], axis=dim)
    return block


def extended(value, sides, width):
    edges = {}
    for axis, dim in sides:
        devices, length = (lax.axis_size(axis), value.shape[dim])
        up = [(i, (i + 1) % devices) for i in range(devices - 1)]
        last = lax.slice_in_dim(value, length - width, length, axis=dim)
        first = lax.slice_in_dim(value, 0, width, axis=dim)
        edges[dim] = (
            lax.ppermute(last, axis, up),
            lax.ppermute(first, axis, [(b, a) for a, b in up]),
        )
    done = []
    for _, dim in sides:
        low, high = edges[dim]
        around = [(width, width) if d in done else (0, 0) for d in range(value.ndim)]
        value = jnp.concatenate([jnp.pad(low, around), value, jnp.pad(high, around)], axis=dim)
        done.append(dim)
    return value


def from_behind(block, axis, distance):
    devices = range(lax.axis_size(axis))
    route = [(i - distance, i) for i in devices if i - distance in devices]
    return lax.ppermute(block, axis, route)


def filled_up(lines, devices):
    spare = -len(lines) % devices
    return jnp.pad(lines, [(0, spare)] + [(0, 0)] * (lines.ndim - 1))


def from_everyone(value, axis):
    devices = lax.axis_size(axis)
    return lax.all_to_all(
        jnp.broadcast_to(value[None], (devices, *value.shape)), axis, 0, 0, tiled=True
    )


def laid_out(pieces, dim):
    dims = list(pieces.shape[1:])
    dims[dim] *= pieces.shape[0]
    return jnp.moveaxis(pieces, 0, dim).reshape(dims)


def whole_of(value, axes, dim):
    far, near = axes
    pieces = from_everyone(from_everyone(value, far), near)
    return laid_out(pieces.swapaxes(0, 1).reshape(-1, *value.shape), dim)


def split_up(value, dim, devices):
    dims = value.shape
    pieces = value.reshape(*dims[:dim], devices, dims[dim] // devices, *dims[dim + 1 :])
    return jnp.moveaxis(pieces, dim, 0)


def sum_at_owner(value, axis, dim):
    devices = lax.axis_size(axis)
    pieces = lax.all_to_all(split_up(value, dim, devices), axis, 0, 0, tiled=True)
    return jnp.sum(pieces, axis=0)


def sum_in_two_steps(value, axes, dim):
    far, near = axes
    own = sum_at_owner(split_up(value, dim, lax.axis_size(far)), near, dim + 1)
    return jnp.sum(lax.all_to_all(own, far, 0, 0, tiled=True), axis=0)


def total_of(value, axes):
    lines = value.reshape(-1, value.shape[-1])
    padded = filled_up(lines, lax.axis_size(axes[0]) * lax.axis_size(axes[1]))
    whole = whole_of(sum_in_two_steps(padded, axes, 0), axes, 0)
    return lax.slice_in_dim(whole, 0, len(lines)).reshape(value.shape)


def total_of_2(value, axes):
    own = sum_in_two_steps(
        filled_up(value, lax.axis_size(axes[0]) * lax.axis_size(axes[1])), axes, 0
    )
    whole = whole_of(own, axes, 0)
    return whole[: len(value)].reshape(value.shape)


def in_one(arrays, axis):
    flat, at, done = (jnp.concatenate([a.reshape(-1) for a in arrays]), 0, [])
    running = total_of_2(flat, axis)
    for a in arrays:
        done.append(running[at : at + a.size].reshape(a.shape))
        at += a.size
    return tuple(done)


def split_parts(packed):
    flipped = jnp.swapaxes(packed, 1, 2)
    return jnp.stack([0.5 * (packed + flipped), 0.5 * (packed - flipped)])


def central(values, which_dim):
    padding = [(0, 0)] * values.ndim
    padding[which_dim] = (1, 1)
    padded = jnp.pad(values, padding)
    extent = values.shape[which_dim]
    return 0.5 * (
        lax.slice_in_dim(padded, 2, extent + 2, axis=which_dim)
        - lax.slice_in_dim(padded, 0, extent, axis=which_dim)
    )


def position_slopes(values):
    padded = padded_2(values, ((GX, 0),), 1)
    along_first = 0.5 * (padded[2:] - padded[:-2])
    return jnp.stack([along_first, central(values, 1), central(values, 2)])


def velocity_slopes(values):
    padded = extended(values, ((GX, 1), ("vert", 0)), 1)
    along_first = 0.5 * (padded[2:, 1:-1] - padded[:-2, 1:-1])
    along_second = 0.5 * (padded[1:-1, 2:] - padded[1:-1, :-2])
    return jnp.stack([along_first, along_second, central(values, 2)])


def coordinate(indices, cell_total):
    return (2.0 * indices.astype(jnp.float32) + 1.0 - cell_total) / cell_total


def velocity_grid(
    offset, slab_cells, first_count, second_offset, second_cells, second_count, third_count
):
    grid_shape = (slab_cells, second_cells, third_count)
    first_axis = coordinate(offset + jnp.arange(slab_cells, dtype=jnp.int32), first_count)
    second_axis = coordinate(
        second_offset + jnp.arange(second_cells, dtype=jnp.int32), second_count
    )
    third_axis = coordinate(jnp.arange(third_count, dtype=jnp.int32), third_count)
    return jnp.stack(
        [
            jnp.broadcast_to(first_axis[:, None, None], grid_shape),
            jnp.broadcast_to(second_axis[None, :, None], grid_shape),
            third_axis[None, None, :],
        ]
    )


def moments(factor, others, cells_count):
    return jnp.einsum("xyzr,dxyzs->drs", factor, others, precision=HIGHEST) / cells_count


def apply_pair(first_terms, first_mats, second_terms, second_mats):
    return -(
        jnp.einsum("dxyzs,drs->xyzr", first_terms, first_mats, precision=HIGHEST)
        + jnp.einsum("dxyzs,drs->xyzr", second_terms, second_mats, precision=HIGHEST)
    )


def newton_schulz(gram_matrix):
    frob_norm = jnp.sqrt(jnp.sum(gram_matrix * gram_matrix) + NORM_EPSILON)
    identity = jnp.eye(gram_matrix.shape[0], dtype=jnp.float32)
    root_part = gram_matrix / frob_norm
    inv_root = identity
    for sweep_index in range(NS_STEPS):
        middle = 1.5 * identity - 0.5 * jnp.dot(
            inv_root, root_part, precision=HIGHEST, preferred_element_type=jnp.float32
        )
        root_part = jnp.dot(
            root_part, middle, precision=HIGHEST, preferred_element_type=jnp.float32
        )
        inv_root = jnp.dot(middle, inv_root, precision=HIGHEST, preferred_element_type=jnp.float32)
    scale_root = jnp.sqrt(frob_norm)
    return (inv_root / scale_root, root_part * scale_root)


def sandwich(left_mats, core_matrix, right_mats):
    return jnp.einsum("dij,jk,dlk->il", left_mats, core_matrix, right_mats, precision=HIGHEST)


def per_device(position_factor, coefficients, velocity_factor, gravity):
    slab_vel = velocity_factor.shape[0]
    column_vel = velocity_factor.shape[1]
    first_count = slab_vel * lax.axis_size("vert")
    second_count = column_vel * lax.axis_size(GX)
    pos_cells = (
        position_factor.shape[0]
        * lax.axis_size(GX)
        * position_factor.shape[1]
        * position_factor.shape[2]
    )
    vel_cells = first_count * second_count * velocity_factor.shape[2]
    offset = lax.axis_index("vert") * slab_vel
    second_offset = lax.axis_index(GX) * column_vel
    velocity = velocity_grid(
        offset,
        slab_vel,
        first_count,
        second_offset,
        column_vel,
        second_count,
        velocity_factor.shape[2],
    )
    vel_first = moments(velocity_factor, velocity[..., None] * velocity_factor[None], vel_cells)
    next_plane = from_behind(velocity_factor, "vert", -1)
    next_column = from_behind(velocity_factor, GX, -1)
    following = jnp.concatenate([velocity_factor[1:], next_plane], axis=0)
    beside = jnp.concatenate([velocity_factor[:, 1:], next_column], axis=1)
    pair_sums = jnp.stack(
        [
            jnp.einsum("xyzr,xyzs->rs", velocity_factor, following, precision=HIGHEST),
            jnp.einsum("xyzr,xyzs->rs", velocity_factor, beside, precision=HIGHEST),
            jnp.einsum(
                "xyzr,xyzs->rs",
                velocity_factor[:, :, :-1],
                velocity_factor[:, :, 1:],
                precision=HIGHEST,
            ),
        ]
    )
    vel_second = 0.5 * (pair_sums - jnp.swapaxes(pair_sums, 1, 2)) / vel_cells
    vel_packed = (vel_first + vel_second).reshape(-1)
    vel_mats = split_parts(
        total_of_2(vel_packed, (("gx_0", "gx_1"), ("gx_2", "vert"))).reshape(vel_first.shape)
    )

    def position_rate(values):
        return apply_pair(
            position_slopes(values), vel_mats[0], gravity[..., None] * values[None], vel_mats[1]
        )

    initial = jnp.einsum("xyzs,sr->xyzr", position_factor, coefficients, precision=HIGHEST)
    section_one = initial + TIME_STEP * position_rate(initial)
    section_two = 0.75 * initial + 0.25 * (section_one + TIME_STEP * position_rate(section_one))
    final_section = 1.0 / 3.0 * initial + 2.0 / 3.0 * (
        section_two + TIME_STEP * position_rate(section_two)
    )
    gram_part = (
        jnp.einsum("xyzr,xyzs->rs", final_section, final_section, precision=HIGHEST) / pos_cells
    )
    raw_terms = jnp.stack(
        [
            moments(final_section, position_slopes(final_section), pos_cells),
            moments(final_section, gravity[..., None] * final_section[None], pos_cells),
        ]
    )
    local_packed = jnp.concatenate([gram_part[None], raw_terms[0] + raw_terms[1]])
    packed = total_of_2(local_packed.reshape(-1), (("gx_0", "gx_1"), "gx_2")).reshape(
        local_packed.shape
    )
    gram_matrix = 0.5 * (packed[0] + packed[0].T)
    second_raw, first_raw = split_parts(packed[1:])
    summed_terms = jnp.stack([first_raw, second_raw])
    inv_root, root_part = newton_schulz(gram_matrix)
    new_position = jnp.einsum("xyzs,sr->xyzr", final_section, inv_root, precision=HIGHEST)
    pos_mats = jnp.einsum("ir,ndij,js->ndrs", inv_root, summed_terms, inv_root, precision=HIGHEST)
    coupled_core = root_part + TIME_STEP * (
        sandwich(pos_mats[0], root_part, vel_mats[0])
        + sandwich(pos_mats[1], root_part, vel_mats[1])
    )

    def velocity_rate(values):
        return apply_pair(
            velocity[..., None] * values[None], pos_mats[0], velocity_slopes(values), pos_mats[1]
        )

    vel_initial = jnp.einsum("abcs,rs->abcr", velocity_factor, coupled_core, precision=HIGHEST)
    vel_section = vel_initial + TIME_STEP * velocity_rate(vel_initial)
    new_velocity = 0.5 * vel_initial + 0.5 * (vel_section + TIME_STEP * velocity_rate(vel_section))
    return (new_position, new_velocity)


def solution(mesh):
    finer = Mesh(
        mesh.devices.reshape(8, 4, 2, mesh.shape["vert"]), ("gx_0", "gx_1", "gx_2", "vert")
    )
    in_specs = (P(GX, None, None, None), P(), P("vert", GX, None, None), P(None, GX, None, None))
    out_specs = (P(GX, None, None, None), P("vert", GX, None, None))
    return jax.shard_map(
        per_device, mesh=finer, in_specs=in_specs, out_specs=out_specs, check_vma=False
    )
```

```python
import jax
import jax.numpy as jnp
from jax import lax
from jax.sharding import Mesh
from jax.sharding import PartitionSpec as P

NS_STEPS = 8
GX = ("gx_0", "gx_1", "gx_2")


HIGHEST = lax.Precision.HIGHEST
TIME_STEP = 0.25
NORM_EPSILON = 1e-06


def padded_2(block, sides, width):
    for axis, dim in sides:
        count = lax.axis_size(axis)
        forward = [(i, i + 1) for i in range(count - 1)]
        backward = [(target, source) for source, target in forward]
        low = lax.ppermute(
            lax.slice_in_dim(block, block.shape[dim] - width, None, axis=dim), axis, forward
        )
        high = lax.ppermute(lax.slice_in_dim(block, 0, width, axis=dim), axis, backward)
        block = jnp.concatenate([low, block, high], axis=dim)
    return block


def extended(value, sides, width):
    edges = {}
    for axis, dim in sides:
        devices, length = (lax.axis_size(axis), value.shape[dim])
        up = [(i, (i + 1) % devices) for i in range(devices - 1)]
        last = lax.slice_in_dim(value, length - width, length, axis=dim)
        first = lax.slice_in_dim(value, 0, width, axis=dim)
        edges[dim] = (
            lax.ppermute(last, axis, up),
            lax.ppermute(first, axis, [(b, a) for a, b in up]),
        )
    done = []
    for _, dim in sides:
        low, high = edges[dim]
        around = [(width, width) if d in done else (0, 0) for d in range(value.ndim)]
        value = jnp.concatenate([jnp.pad(low, around), value, jnp.pad(high, around)], axis=dim)
        done.append(dim)
    return value


def from_behind(block, axis, distance):
    devices = range(lax.axis_size(axis))
    route = [(i - distance, i) for i in devices if i - distance in devices]
    return lax.ppermute(block, axis, route)


def filled_up(lines, devices):
    spare = -len(lines) % devices
    return jnp.pad(lines, [(0, spare)] + [(0, 0)] * (lines.ndim - 1))


def from_everyone(value, axis):
    devices = lax.axis_size(axis)
    return lax.all_to_all(
        jnp.broadcast_to(value[None], (devices, *value.shape)), axis, 0, 0, tiled=True
    )


def laid_out(pieces, dim):
    dims = list(pieces.shape[1:])
    dims[dim] *= pieces.shape[0]
    return jnp.moveaxis(pieces, 0, dim).reshape(dims)


def whole_of(value, axes, dim):
    far, near = axes
    pieces = from_everyone(from_everyone(value, far), near)
    return laid_out(pieces.swapaxes(0, 1).reshape(-1, *value.shape), dim)


def split_up(value, dim, devices):
    dims = value.shape
    pieces = value.reshape(*dims[:dim], devices, dims[dim] // devices, *dims[dim + 1 :])
    return jnp.moveaxis(pieces, dim, 0)


def sum_at_owner(value, axis, dim):
    devices = lax.axis_size(axis)
    pieces = lax.all_to_all(split_up(value, dim, devices), axis, 0, 0, tiled=True)
    return jnp.sum(pieces, axis=0)


def sum_in_two_steps(value, axes, dim):
    far, near = axes
    own = sum_at_owner(split_up(value, dim, lax.axis_size(far)), near, dim + 1)
    return jnp.sum(lax.all_to_all(own, far, 0, 0, tiled=True), axis=0)


def total_of(value, axes):
    lines = value.reshape(-1, value.shape[-1])
    padded = filled_up(lines, lax.axis_size(axes[0]) * lax.axis_size(axes[1]))
    whole = whole_of(sum_in_two_steps(padded, axes, 0), axes, 0)
    return lax.slice_in_dim(whole, 0, len(lines)).reshape(value.shape)


def total_of_2(value, axes):
    own = sum_in_two_steps(
        filled_up(value, lax.axis_size(axes[0]) * lax.axis_size(axes[1])), axes, 0
    )
    whole = whole_of(own, axes, 0)
    return whole[: len(value)].reshape(value.shape)


def in_one(arrays, axis):
    flat, at, done = (jnp.concatenate([a.reshape(-1) for a in arrays]), 0, [])
    running = total_of_2(flat, axis)
    for a in arrays:
        done.append(running[at : at + a.size].reshape(a.shape))
        at += a.size
    return tuple(done)


def staged_total(flat, axes):
    sizes = [lax.axis_size(a) for a in axes]
    devices = 1
    for n in sizes:
        devices *= n
    length = flat.shape[0]
    piece = -(-length // (devices * 128)) * 128
    part = jnp.pad(flat, (0, piece * devices - length))
    for axis, n in zip(axes, sizes):
        rows = part.reshape(n, -1, 128)
        part = jnp.sum(lax.all_to_all(rows, axis, 0, 0, tiled=True), axis=0).reshape(-1)
    for axis, n in zip(axes[::-1], sizes[::-1]):
        rows = jnp.broadcast_to(part.reshape(1, -1, 128), (n, part.shape[0] // 128, 128))
        part = lax.all_to_all(rows, axis, 0, 0, tiled=True).reshape(-1)
    return part[:length]


def split_parts(packed):
    flipped = jnp.swapaxes(packed, 1, 2)
    return jnp.stack([0.5 * (packed + flipped), 0.5 * (packed - flipped)])


def central(values, which_dim):
    padding = [(0, 0)] * values.ndim
    padding[which_dim] = (1, 1)
    padded = jnp.pad(values, padding)
    extent = values.shape[which_dim]
    return 0.5 * (
        lax.slice_in_dim(padded, 2, extent + 2, axis=which_dim)
        - lax.slice_in_dim(padded, 0, extent, axis=which_dim)
    )


def position_slopes(values):
    padded = padded_2(values, ((GX, 0),), 1)
    along_first = 0.5 * (padded[2:] - padded[:-2])
    return jnp.stack([along_first, central(values, 1), central(values, 2)])


def velocity_slopes(values):
    padded = extended(values, ((GX, 1), ("vert", 0)), 1)
    along_first = 0.5 * (padded[2:, 1:-1] - padded[:-2, 1:-1])
    along_second = 0.5 * (padded[1:-1, 2:] - padded[1:-1, :-2])
    return jnp.stack([along_first, along_second, central(values, 2)])


def coordinate(indices, cell_total):
    return (2.0 * indices.astype(jnp.float32) + 1.0 - cell_total) / cell_total


def velocity_grid(
    offset, slab_cells, first_count, second_offset, second_cells, second_count, third_count
):
    grid_shape = (slab_cells, second_cells, third_count)
    first_axis = coordinate(offset + jnp.arange(slab_cells, dtype=jnp.int32), first_count)
    second_axis = coordinate(
        second_offset + jnp.arange(second_cells, dtype=jnp.int32), second_count
    )
    third_axis = coordinate(jnp.arange(third_count, dtype=jnp.int32), third_count)
    return jnp.stack(
        [
            jnp.broadcast_to(first_axis[:, None, None], grid_shape),
            jnp.broadcast_to(second_axis[None, :, None], grid_shape),
            third_axis[None, None, :],
        ]
    )


def moments(factor, others, cells_count):
    return jnp.einsum("xyzr,dxyzs->drs", factor, others, precision=HIGHEST) / cells_count


def apply_pair(first_terms, first_mats, second_terms, second_mats):
    return -(
        jnp.einsum("dxyzs,drs->xyzr", first_terms, first_mats, precision=HIGHEST)
        + jnp.einsum("dxyzs,drs->xyzr", second_terms, second_mats, precision=HIGHEST)
    )


def newton_schulz(gram_matrix):
    frob_norm = jnp.sqrt(jnp.sum(gram_matrix * gram_matrix) + NORM_EPSILON)
    identity = jnp.eye(gram_matrix.shape[0], dtype=jnp.float32)
    root_part = gram_matrix / frob_norm
    inv_root = identity
    for sweep_index in range(NS_STEPS):
        middle = 1.5 * identity - 0.5 * jnp.dot(
            inv_root, root_part, precision=HIGHEST, preferred_element_type=jnp.float32
        )
        root_part = jnp.dot(
            root_part, middle, precision=HIGHEST, preferred_element_type=jnp.float32
        )
        inv_root = jnp.dot(middle, inv_root, precision=HIGHEST, preferred_element_type=jnp.float32)
    scale_root = jnp.sqrt(frob_norm)
    return (inv_root / scale_root, root_part * scale_root)


def sandwich(left_mats, core_matrix, right_mats):
    return jnp.einsum("dij,jk,dlk->il", left_mats, core_matrix, right_mats, precision=HIGHEST)


def per_device(position_factor, coefficients, velocity_factor, gravity):
    slab_vel = velocity_factor.shape[0]
    column_vel = velocity_factor.shape[1]
    first_count = slab_vel * lax.axis_size("vert")
    second_count = column_vel * lax.axis_size(GX)
    pos_cells = (
        position_factor.shape[0]
        * lax.axis_size(GX)
        * position_factor.shape[1]
        * position_factor.shape[2]
    )
    vel_cells = first_count * second_count * velocity_factor.shape[2]
    offset = lax.axis_index("vert") * slab_vel
    second_offset = lax.axis_index(GX) * column_vel
    velocity = velocity_grid(
        offset,
        slab_vel,
        first_count,
        second_offset,
        column_vel,
        second_count,
        velocity_factor.shape[2],
    )
    vel_first = moments(velocity_factor, velocity[..., None] * velocity_factor[None], vel_cells)
    next_plane = from_behind(velocity_factor, "vert", -1)
    next_column = from_behind(velocity_factor, GX, -1)
    following = jnp.concatenate([velocity_factor[1:], next_plane], axis=0)
    beside = jnp.concatenate([velocity_factor[:, 1:], next_column], axis=1)
    pair_sums = jnp.stack(
        [
            jnp.einsum("xyzr,xyzs->rs", velocity_factor, following, precision=HIGHEST),
            jnp.einsum("xyzr,xyzs->rs", velocity_factor, beside, precision=HIGHEST),
            jnp.einsum(
                "xyzr,xyzs->rs",
                velocity_factor[:, :, :-1],
                velocity_factor[:, :, 1:],
                precision=HIGHEST,
            ),
        ]
    )
    vel_second = 0.5 * (pair_sums - jnp.swapaxes(pair_sums, 1, 2)) / vel_cells
    vel_packed = (vel_first + vel_second).reshape(-1)
    vel_mats = split_parts(
        staged_total(vel_packed, ("gx_2", "gx_1", "vert", "gx_0")).reshape(vel_first.shape)
    )

    def position_rate(values):
        return apply_pair(
            position_slopes(values), vel_mats[0], gravity[..., None] * values[None], vel_mats[1]
        )

    initial = jnp.einsum("xyzs,sr->xyzr", position_factor, coefficients, precision=HIGHEST)
    section_one = initial + TIME_STEP * position_rate(initial)
    section_two = 0.75 * initial + 0.25 * (section_one + TIME_STEP * position_rate(section_one))
    final_section = 1.0 / 3.0 * initial + 2.0 / 3.0 * (
        section_two + TIME_STEP * position_rate(section_two)
    )
    gram_part = (
        jnp.einsum("xyzr,xyzs->rs", final_section, final_section, precision=HIGHEST) / pos_cells
    )
    raw_terms = jnp.stack(
        [
            moments(final_section, position_slopes(final_section), pos_cells),
            moments(final_section, gravity[..., None] * final_section[None], pos_cells),
        ]
    )
    local_packed = jnp.concatenate([gram_part[None], raw_terms[0] + raw_terms[1]])
    packed = staged_total(local_packed.reshape(-1), ("gx_2", "gx_1", "gx_0")).reshape(
        local_packed.shape
    )
    gram_matrix = 0.5 * (packed[0] + packed[0].T)
    second_raw, first_raw = split_parts(packed[1:])
    summed_terms = jnp.stack([first_raw, second_raw])
    inv_root, root_part = newton_schulz(gram_matrix)
    new_position = jnp.einsum("xyzs,sr->xyzr", final_section, inv_root, precision=HIGHEST)
    pos_mats = jnp.einsum("ir,ndij,js->ndrs", inv_root, summed_terms, inv_root, precision=HIGHEST)
    coupled_core = root_part + TIME_STEP * (
        sandwich(pos_mats[0], root_part, vel_mats[0])
        + sandwich(pos_mats[1], root_part, vel_mats[1])
    )

    def velocity_rate(values):
        return apply_pair(
            velocity[..., None] * values[None], pos_mats[0], velocity_slopes(values), pos_mats[1]
        )

    vel_initial = jnp.einsum("abcs,rs->abcr", velocity_factor, coupled_core, precision=HIGHEST)
    vel_section = vel_initial + TIME_STEP * velocity_rate(vel_initial)
    new_velocity = 0.5 * vel_initial + 0.5 * (vel_section + TIME_STEP * velocity_rate(vel_section))
    return (new_position, new_velocity)


def solution(mesh):
    finer = Mesh(
        mesh.devices.reshape(8, 4, 2, mesh.shape["vert"]), ("gx_0", "gx_1", "gx_2", "vert")
    )
    in_specs = (P(GX, None, None, None), P(), P("vert", GX, None, None), P(None, GX, None, None))
    out_specs = (P(GX, None, None, None), P("vert", GX, None, None))
    return jax.shard_map(
        per_device, mesh=finer, in_specs=in_specs, out_specs=out_specs, check_vma=False
    )
```

```python
import jax
import jax.numpy as jnp
from jax import lax
from jax.sharding import Mesh
from jax.sharding import PartitionSpec as P

NS_STEPS = 8
GX = ("gx_0", "gx_1", "gx_2")


HIGHEST = lax.Precision.HIGHEST
TIME_STEP = 0.25
NORM_EPSILON = 1e-06


def padded_2(block, sides, width):
    for axis, dim in sides:
        count = lax.axis_size(axis)
        forward = [(i, i + 1) for i in range(count - 1)]
        backward = [(target, source) for source, target in forward]
        low = lax.ppermute(
            lax.slice_in_dim(block, block.shape[dim] - width, None, axis=dim), axis, forward
        )
        high = lax.ppermute(lax.slice_in_dim(block, 0, width, axis=dim), axis, backward)
        block = jnp.concatenate([low, block, high], axis=dim)
    return block


def extended(value, sides, width):
    edges = {}
    for axis, dim in sides:
        devices, length = (lax.axis_size(axis), value.shape[dim])
        up = [(i, (i + 1) % devices) for i in range(devices - 1)]
        last = lax.slice_in_dim(value, length - width, length, axis=dim)
        first = lax.slice_in_dim(value, 0, width, axis=dim)
        edges[dim] = (
            lax.ppermute(last, axis, up),
            lax.ppermute(first, axis, [(b, a) for a, b in up]),
        )
    done = []
    for _, dim in sides:
        low, high = edges[dim]
        around = [(width, width) if d in done else (0, 0) for d in range(value.ndim)]
        value = jnp.concatenate([jnp.pad(low, around), value, jnp.pad(high, around)], axis=dim)
        done.append(dim)
    return value


def from_behind(block, axis, distance):
    devices = range(lax.axis_size(axis))
    route = [(i - distance, i) for i in devices if i - distance in devices]
    return lax.ppermute(block, axis, route)


def filled_up(lines, devices):
    spare = -len(lines) % devices
    return jnp.pad(lines, [(0, spare)] + [(0, 0)] * (lines.ndim - 1))


def from_everyone(value, axis):
    devices = lax.axis_size(axis)
    return lax.all_to_all(
        jnp.broadcast_to(value[None], (devices, *value.shape)), axis, 0, 0, tiled=True
    )


def laid_out(pieces, dim):
    dims = list(pieces.shape[1:])
    dims[dim] *= pieces.shape[0]
    return jnp.moveaxis(pieces, 0, dim).reshape(dims)


def whole_of(value, axes, dim):
    far, near = axes
    pieces = from_everyone(from_everyone(value, far), near)
    return laid_out(pieces.swapaxes(0, 1).reshape(-1, *value.shape), dim)


def split_up(value, dim, devices):
    dims = value.shape
    pieces = value.reshape(*dims[:dim], devices, dims[dim] // devices, *dims[dim + 1 :])
    return jnp.moveaxis(pieces, dim, 0)


def sum_at_owner(value, axis, dim):
    devices = lax.axis_size(axis)
    pieces = lax.all_to_all(split_up(value, dim, devices), axis, 0, 0, tiled=True)
    return jnp.sum(pieces, axis=0)


def sum_in_two_steps(value, axes, dim):
    far, near = axes
    own = sum_at_owner(split_up(value, dim, lax.axis_size(far)), near, dim + 1)
    return jnp.sum(lax.all_to_all(own, far, 0, 0, tiled=True), axis=0)


def total_of(value, axes):
    lines = value.reshape(-1, value.shape[-1])
    padded = filled_up(lines, lax.axis_size(axes[0]) * lax.axis_size(axes[1]))
    whole = whole_of(sum_in_two_steps(padded, axes, 0), axes, 0)
    return lax.slice_in_dim(whole, 0, len(lines)).reshape(value.shape)


def total_of_2(value, axes):
    own = sum_in_two_steps(
        filled_up(value, lax.axis_size(axes[0]) * lax.axis_size(axes[1])), axes, 0
    )
    whole = whole_of(own, axes, 0)
    return whole[: len(value)].reshape(value.shape)


def in_one(arrays, axis):
    flat, at, done = (jnp.concatenate([a.reshape(-1) for a in arrays]), 0, [])
    running = total_of_2(flat, axis)
    for a in arrays:
        done.append(running[at : at + a.size].reshape(a.shape))
        at += a.size
    return tuple(done)


def staged_total(flat, axes):
    sizes = [lax.axis_size(a) for a in axes]
    devices = 1
    for n in sizes:
        devices *= n
    length = flat.shape[0]
    piece = -(-length // (devices * 128)) * 128
    part = jnp.pad(flat, (0, piece * devices - length))
    for axis, n in zip(axes, sizes):
        rows = part.reshape(n, -1, 128)
        part = jnp.sum(lax.all_to_all(rows, axis, 0, 0, tiled=True), axis=0).reshape(-1)
    for axis, n in zip(axes[::-1], sizes[::-1]):
        rows = jnp.broadcast_to(part.reshape(1, -1, 128), (n, part.shape[0] // 128, 128))
        part = lax.all_to_all(rows, axis, 0, 0, tiled=True).reshape(-1)
    return part[:length]


CROSS = ((1, 0), (-1, 0), (0, 1), (0, -1))


def local_velocity_update(around, core, pos_mats, first_count, second_count, shape):
    a = lax.axis_index("vert")
    b = lax.axis_index(GX)
    offsets = list(around)
    blocks = jnp.stack([around[o].reshape(shape[2], shape[3]) for o in offsets])
    levels = jnp.einsum("nxs,rs->nxr", blocks, core, precision=HIGHEST)
    cells = shape[2]
    third = coordinate(jnp.arange(cells, dtype=jnp.int32), cells)[:, None]

    def combine(centre, first, second, along, first_pos, second_pos):
        terms = jnp.stack(
            [
                coordinate(first_pos, first_count)[..., None, None] * centre,
                coordinate(second_pos, second_count)[..., None, None] * centre,
                third * centre,
                first,
                second,
                along,
            ]
        )
        return -(
            jnp.einsum("dnxs,drs->nxr", terms[:3], pos_mats[0], precision=HIGHEST)
            + jnp.einsum("dnxs,drs->nxr", terms[3:], pos_mats[1], precision=HIGHEST)
        )

    inner = [(0, 0), *CROSS]
    index = {o: i for i, o in enumerate(offsets)}
    by_shift = {
        s: jnp.stack([levels[index[(o[0] + s[0], o[1] + s[1])]] for o in inner])
        for s in [(0, 0), *CROSS]
    }
    centre = by_shift[(0, 0)]
    first = 0.5 * (by_shift[(1, 0)] - by_shift[(-1, 0)])
    second = 0.5 * (by_shift[(0, 1)] - by_shift[(0, -1)])
    padded = jnp.pad(centre, ((0, 0), (1, 1), (0, 0)))
    along = 0.5 * (padded[:, 2:] - padded[:, :-2])
    rows = jnp.array([o[0] for o in inner]) + a
    cols = jnp.array([o[1] for o in inner]) + b
    inside = (rows >= 0) & (rows < first_count) & (cols >= 0) & (cols < second_count)
    staged = centre + TIME_STEP * combine(centre, first, second, along, rows, cols)
    staged = jnp.where(inside[:, None, None], staged, 0.0)
    me = staged[0]
    first = 0.5 * (staged[1] - staged[2])
    second = 0.5 * (staged[3] - staged[4])
    padded = jnp.pad(me, ((1, 1), (0, 0)))
    along = 0.5 * (padded[2:] - padded[:-2])
    last = combine(me[None], first[None], second[None], along[None], a[None], b[None])[0]
    result = 0.5 * centre[0] + 0.5 * (me + TIME_STEP * last)
    return result.reshape(shape)


def split_parts(packed):
    flipped = jnp.swapaxes(packed, 1, 2)
    return jnp.stack([0.5 * (packed + flipped), 0.5 * (packed - flipped)])


def central(values, which_dim):
    padding = [(0, 0)] * values.ndim
    padding[which_dim] = (1, 1)
    padded = jnp.pad(values, padding)
    extent = values.shape[which_dim]
    return 0.5 * (
        lax.slice_in_dim(padded, 2, extent + 2, axis=which_dim)
        - lax.slice_in_dim(padded, 0, extent, axis=which_dim)
    )


def position_slopes(values):
    padded = padded_2(values, ((GX, 0),), 1)
    along_first = 0.5 * (padded[2:] - padded[:-2])
    return jnp.stack([along_first, central(values, 1), central(values, 2)])


def velocity_slopes(values):
    padded = extended(values, ((GX, 1), ("vert", 0)), 1)
    along_first = 0.5 * (padded[2:, 1:-1] - padded[:-2, 1:-1])
    along_second = 0.5 * (padded[1:-1, 2:] - padded[1:-1, :-2])
    return jnp.stack([along_first, along_second, central(values, 2)])


def coordinate(indices, cell_total):
    return (2.0 * indices.astype(jnp.float32) + 1.0 - cell_total) / cell_total


def velocity_grid(
    offset, slab_cells, first_count, second_offset, second_cells, second_count, third_count
):
    grid_shape = (slab_cells, second_cells, third_count)
    first_axis = coordinate(offset + jnp.arange(slab_cells, dtype=jnp.int32), first_count)
    second_axis = coordinate(
        second_offset + jnp.arange(second_cells, dtype=jnp.int32), second_count
    )
    third_axis = coordinate(jnp.arange(third_count, dtype=jnp.int32), third_count)
    return jnp.stack(
        [
            jnp.broadcast_to(first_axis[:, None, None], grid_shape),
            jnp.broadcast_to(second_axis[None, :, None], grid_shape),
            third_axis[None, None, :],
        ]
    )


def moments(factor, others, cells_count):
    return jnp.einsum("xyzr,dxyzs->drs", factor, others, precision=HIGHEST) / cells_count


def apply_pair(first_terms, first_mats, second_terms, second_mats):
    return -(
        jnp.einsum("dxyzs,drs->xyzr", first_terms, first_mats, precision=HIGHEST)
        + jnp.einsum("dxyzs,drs->xyzr", second_terms, second_mats, precision=HIGHEST)
    )


def newton_schulz(gram_matrix):
    frob_norm = jnp.sqrt(jnp.sum(gram_matrix * gram_matrix) + NORM_EPSILON)
    identity = jnp.eye(gram_matrix.shape[0], dtype=jnp.float32)
    root_part = gram_matrix / frob_norm
    inv_root = identity
    for sweep_index in range(NS_STEPS):
        middle = 1.5 * identity - 0.5 * jnp.dot(
            inv_root, root_part, precision=HIGHEST, preferred_element_type=jnp.float32
        )
        root_part = jnp.dot(
            root_part, middle, precision=HIGHEST, preferred_element_type=jnp.float32
        )
        inv_root = jnp.dot(middle, inv_root, precision=HIGHEST, preferred_element_type=jnp.float32)
    scale_root = jnp.sqrt(frob_norm)
    return (inv_root / scale_root, root_part * scale_root)


def sandwich(left_mats, core_matrix, right_mats):
    return jnp.einsum("dij,jk,dlk->il", left_mats, core_matrix, right_mats, precision=HIGHEST)


def per_device(position_factor, coefficients, velocity_factor, gravity):
    slab_vel = velocity_factor.shape[0]
    column_vel = velocity_factor.shape[1]
    first_count = slab_vel * lax.axis_size("vert")
    second_count = column_vel * lax.axis_size(GX)
    pos_cells = (
        position_factor.shape[0]
        * lax.axis_size(GX)
        * position_factor.shape[1]
        * position_factor.shape[2]
    )
    vel_cells = first_count * second_count * velocity_factor.shape[2]
    offset = lax.axis_index("vert") * slab_vel
    second_offset = lax.axis_index(GX) * column_vel
    velocity = velocity_grid(
        offset,
        slab_vel,
        first_count,
        second_offset,
        column_vel,
        second_count,
        velocity_factor.shape[2],
    )
    vel_first = moments(velocity_factor, velocity[..., None] * velocity_factor[None], vel_cells)
    next_plane = from_behind(velocity_factor, "vert", -1)
    next_column = from_behind(velocity_factor, GX, -1)
    around = {(1, 0): next_plane, (0, 1): next_column}
    if slab_vel == 1 and column_vel == 1:
        around[(-1, 0)] = from_behind(velocity_factor, "vert", 1)
        around[(0, -1)] = from_behind(velocity_factor, GX, 1)
        around[(2, 0)] = from_behind(velocity_factor, "vert", -2)
        around[(-2, 0)] = from_behind(velocity_factor, "vert", 2)
        around[(0, 2)] = from_behind(velocity_factor, GX, -2)
        around[(0, -2)] = from_behind(velocity_factor, GX, 2)
        sides = jnp.stack([around[(0, 1)], around[(0, -1)]])
        up_pair = from_behind(sides, "vert", -1)
        down_pair = from_behind(sides, "vert", 1)
        around[(1, 1)], around[(1, -1)] = up_pair[0], up_pair[1]
        around[(-1, 1)], around[(-1, -1)] = down_pair[0], down_pair[1]
        around[(0, 0)] = velocity_factor
    following = jnp.concatenate([velocity_factor[1:], next_plane], axis=0)
    beside = jnp.concatenate([velocity_factor[:, 1:], next_column], axis=1)
    pair_sums = jnp.stack(
        [
            jnp.einsum("xyzr,xyzs->rs", velocity_factor, following, precision=HIGHEST),
            jnp.einsum("xyzr,xyzs->rs", velocity_factor, beside, precision=HIGHEST),
            jnp.einsum(
                "xyzr,xyzs->rs",
                velocity_factor[:, :, :-1],
                velocity_factor[:, :, 1:],
                precision=HIGHEST,
            ),
        ]
    )
    vel_second = 0.5 * (pair_sums - jnp.swapaxes(pair_sums, 1, 2)) / vel_cells
    vel_packed = (vel_first + vel_second).reshape(-1)
    vel_mats = split_parts(
        staged_total(vel_packed, ("gx_2", "gx_1", "vert", "gx_0")).reshape(vel_first.shape)
    )

    def position_rate(values):
        return apply_pair(
            position_slopes(values), vel_mats[0], gravity[..., None] * values[None], vel_mats[1]
        )

    initial = jnp.einsum("xyzs,sr->xyzr", position_factor, coefficients, precision=HIGHEST)
    section_one = initial + TIME_STEP * position_rate(initial)
    section_two = 0.75 * initial + 0.25 * (section_one + TIME_STEP * position_rate(section_one))
    final_section = 1.0 / 3.0 * initial + 2.0 / 3.0 * (
        section_two + TIME_STEP * position_rate(section_two)
    )
    gram_part = (
        jnp.einsum("xyzr,xyzs->rs", final_section, final_section, precision=HIGHEST) / pos_cells
    )
    raw_terms = jnp.stack(
        [
            moments(final_section, position_slopes(final_section), pos_cells),
            moments(final_section, gravity[..., None] * final_section[None], pos_cells),
        ]
    )
    local_packed = jnp.concatenate([gram_part[None], raw_terms[0] + raw_terms[1]])
    packed = staged_total(local_packed.reshape(-1), ("gx_2", "gx_1", "gx_0")).reshape(
        local_packed.shape
    )
    gram_matrix = 0.5 * (packed[0] + packed[0].T)
    second_raw, first_raw = split_parts(packed[1:])
    summed_terms = jnp.stack([first_raw, second_raw])
    inv_root, root_part = newton_schulz(gram_matrix)
    new_position = jnp.einsum("xyzs,sr->xyzr", final_section, inv_root, precision=HIGHEST)
    pos_mats = jnp.einsum("ir,ndij,js->ndrs", inv_root, summed_terms, inv_root, precision=HIGHEST)
    coupled_core = root_part + TIME_STEP * (
        sandwich(pos_mats[0], root_part, vel_mats[0])
        + sandwich(pos_mats[1], root_part, vel_mats[1])
    )

    def velocity_rate(values):
        return apply_pair(
            velocity[..., None] * values[None], pos_mats[0], velocity_slopes(values), pos_mats[1]
        )

    if slab_vel != 1 or column_vel != 1:
        vel_initial = jnp.einsum("abcs,rs->abcr", velocity_factor, coupled_core, precision=HIGHEST)
        vel_section = vel_initial + TIME_STEP * velocity_rate(vel_initial)
        new_velocity = 0.5 * vel_initial + 0.5 * (
            vel_section + TIME_STEP * velocity_rate(vel_section)
        )
        return (new_position, new_velocity)
    new_velocity = local_velocity_update(
        around, coupled_core, pos_mats, first_count, second_count, velocity_factor.shape
    )
    return (new_position, new_velocity)


def solution(mesh):
    finer = Mesh(
        mesh.devices.reshape(8, 4, 2, mesh.shape["vert"]), ("gx_0", "gx_1", "gx_2", "vert")
    )
    in_specs = (P(GX, None, None, None), P(), P("vert", GX, None, None), P(None, GX, None, None))
    out_specs = (P(GX, None, None, None), P("vert", GX, None, None))
    return jax.shard_map(
        per_device, mesh=finer, in_specs=in_specs, out_specs=out_specs, check_vma=False
    )
```

```python
import jax
import jax.numpy as jnp
from jax import lax
from jax.sharding import Mesh
from jax.sharding import PartitionSpec as P

NS_STEPS = 8
GX = ("gx_0", "gx_1", "gx_2")


HIGHEST = lax.Precision.HIGHEST
TIME_STEP = 0.25
NORM_EPSILON = 1e-06


def padded_2(block, sides, width):
    for axis, dim in sides:
        count = lax.axis_size(axis)
        forward = [(i, i + 1) for i in range(count - 1)]
        backward = [(target, source) for source, target in forward]
        low = lax.ppermute(
            lax.slice_in_dim(block, block.shape[dim] - width, None, axis=dim), axis, forward
        )
        high = lax.ppermute(lax.slice_in_dim(block, 0, width, axis=dim), axis, backward)
        block = jnp.concatenate([low, block, high], axis=dim)
    return block


def extended(value, sides, width):
    edges = {}
    for axis, dim in sides:
        devices, length = (lax.axis_size(axis), value.shape[dim])
        up = [(i, (i + 1) % devices) for i in range(devices - 1)]
        last = lax.slice_in_dim(value, length - width, length, axis=dim)
        first = lax.slice_in_dim(value, 0, width, axis=dim)
        edges[dim] = (
            lax.ppermute(last, axis, up),
            lax.ppermute(first, axis, [(b, a) for a, b in up]),
        )
    done = []
    for _, dim in sides:
        low, high = edges[dim]
        around = [(width, width) if d in done else (0, 0) for d in range(value.ndim)]
        value = jnp.concatenate([jnp.pad(low, around), value, jnp.pad(high, around)], axis=dim)
        done.append(dim)
    return value


def from_behind(block, axis, distance):
    devices = range(lax.axis_size(axis))
    route = [(i - distance, i) for i in devices if i - distance in devices]
    return lax.ppermute(block, axis, route)


def filled_up(lines, devices):
    spare = -len(lines) % devices
    return jnp.pad(lines, [(0, spare)] + [(0, 0)] * (lines.ndim - 1))


def from_everyone(value, axis):
    devices = lax.axis_size(axis)
    return lax.all_to_all(
        jnp.broadcast_to(value[None], (devices, *value.shape)), axis, 0, 0, tiled=True
    )


def laid_out(pieces, dim):
    dims = list(pieces.shape[1:])
    dims[dim] *= pieces.shape[0]
    return jnp.moveaxis(pieces, 0, dim).reshape(dims)


def whole_of(value, axes, dim):
    far, near = axes
    pieces = from_everyone(from_everyone(value, far), near)
    return laid_out(pieces.swapaxes(0, 1).reshape(-1, *value.shape), dim)


def split_up(value, dim, devices):
    dims = value.shape
    pieces = value.reshape(*dims[:dim], devices, dims[dim] // devices, *dims[dim + 1 :])
    return jnp.moveaxis(pieces, dim, 0)


def sum_at_owner(value, axis, dim):
    devices = lax.axis_size(axis)
    pieces = lax.all_to_all(split_up(value, dim, devices), axis, 0, 0, tiled=True)
    return jnp.sum(pieces, axis=0)


def sum_in_two_steps(value, axes, dim):
    far, near = axes
    own = sum_at_owner(split_up(value, dim, lax.axis_size(far)), near, dim + 1)
    return jnp.sum(lax.all_to_all(own, far, 0, 0, tiled=True), axis=0)


def total_of(value, axes):
    lines = value.reshape(-1, value.shape[-1])
    padded = filled_up(lines, lax.axis_size(axes[0]) * lax.axis_size(axes[1]))
    whole = whole_of(sum_in_two_steps(padded, axes, 0), axes, 0)
    return lax.slice_in_dim(whole, 0, len(lines)).reshape(value.shape)


def total_of_2(value, axes):
    own = sum_in_two_steps(
        filled_up(value, lax.axis_size(axes[0]) * lax.axis_size(axes[1])), axes, 0
    )
    whole = whole_of(own, axes, 0)
    return whole[: len(value)].reshape(value.shape)


def in_one(arrays, axis):
    flat, at, done = (jnp.concatenate([a.reshape(-1) for a in arrays]), 0, [])
    running = total_of_2(flat, axis)
    for a in arrays:
        done.append(running[at : at + a.size].reshape(a.shape))
        at += a.size
    return tuple(done)


def staged_total(flat, axes):
    sizes = [lax.axis_size(a) for a in axes]
    devices = 1
    for n in sizes:
        devices *= n
    length = flat.shape[0]
    piece = -(-length // (devices * 128)) * 128
    part = jnp.pad(flat, (0, piece * devices - length))
    for axis, n in zip(axes, sizes):
        rows = part.reshape(n, -1, 128)
        part = jnp.sum(lax.all_to_all(rows, axis, 0, 0, tiled=True), axis=0).reshape(-1)
    for axis, n in zip(axes[::-1], sizes[::-1]):
        rows = jnp.broadcast_to(part.reshape(1, -1, 128), (n, part.shape[0] // 128, 128))
        part = lax.all_to_all(rows, axis, 0, 0, tiled=True).reshape(-1)
    return part[:length]


def plane_rate(values, grav, vel_mats):
    inner = values[1:-1]
    slopes = jnp.stack(
        [0.5 * (values[2:] - values[:-2]), central(inner, 1), central(inner, 2)]
    )
    pulled = jnp.stack([grav[:, d, :, :, None] * inner for d in range(grav.shape[1])])
    return -(
        jnp.einsum("dnyzs,drs->nyzr", slopes, vel_mats[0], precision=HIGHEST)
        + jnp.einsum("dnyzs,drs->nyzr", pulled, vel_mats[1], precision=HIGHEST)
    )


def local_position_steps(pos_planes, grav_planes, coefficients, vel_mats):
    x = lax.axis_index(GX)
    planes = lax.axis_size(GX)

    def inside(reach):
        at = jnp.arange(-reach, reach + 1) + x
        return ((at >= 0) & (at < planes))[:, None, None, None]

    initial = jnp.einsum("nyzs,sr->nyzr", pos_planes, coefficients, precision=HIGHEST)
    one = initial[1:-1] + TIME_STEP * plane_rate(initial, grav_planes, vel_mats)
    one = jnp.where(inside(3), one, 0.0)
    two = 0.75 * initial[2:-2] + 0.25 * (
        one[1:-1] + TIME_STEP * plane_rate(one, grav_planes[1:-1], vel_mats)
    )
    two = jnp.where(inside(2), two, 0.0)
    three = 1.0 / 3.0 * initial[3:-3] + 2.0 / 3.0 * (
        two[1:-1] + TIME_STEP * plane_rate(two, grav_planes[2:-2], vel_mats)
    )
    return jnp.where(inside(1), three, 0.0)


CROSS = ((1, 0), (-1, 0), (0, 1), (0, -1))


def local_velocity_update(around, core, pos_mats, first_count, second_count, shape):
    a = lax.axis_index("vert")
    b = lax.axis_index(GX)
    offsets = list(around)
    blocks = jnp.stack([around[o].reshape(shape[2], shape[3]) for o in offsets])
    levels = jnp.einsum("nxs,rs->nxr", blocks, core, precision=HIGHEST)
    cells = shape[2]
    third = coordinate(jnp.arange(cells, dtype=jnp.int32), cells)[:, None]

    def combine(centre, first, second, along, first_pos, second_pos):
        terms = jnp.stack(
            [
                coordinate(first_pos, first_count)[..., None, None] * centre,
                coordinate(second_pos, second_count)[..., None, None] * centre,
                third * centre,
                first,
                second,
                along,
            ]
        )
        return -(
            jnp.einsum("dnxs,drs->nxr", terms[:3], pos_mats[0], precision=HIGHEST)
            + jnp.einsum("dnxs,drs->nxr", terms[3:], pos_mats[1], precision=HIGHEST)
        )

    inner = [(0, 0), *CROSS]
    index = {o: i for i, o in enumerate(offsets)}
    by_shift = {
        s: jnp.stack([levels[index[(o[0] + s[0], o[1] + s[1])]] for o in inner])
        for s in [(0, 0), *CROSS]
    }
    centre = by_shift[(0, 0)]
    first = 0.5 * (by_shift[(1, 0)] - by_shift[(-1, 0)])
    second = 0.5 * (by_shift[(0, 1)] - by_shift[(0, -1)])
    padded = jnp.pad(centre, ((0, 0), (1, 1), (0, 0)))
    along = 0.5 * (padded[:, 2:] - padded[:, :-2])
    rows = jnp.array([o[0] for o in inner]) + a
    cols = jnp.array([o[1] for o in inner]) + b
    inside = (rows >= 0) & (rows < first_count) & (cols >= 0) & (cols < second_count)
    staged = centre + TIME_STEP * combine(centre, first, second, along, rows, cols)
    staged = jnp.where(inside[:, None, None], staged, 0.0)
    me = staged[0]
    first = 0.5 * (staged[1] - staged[2])
    second = 0.5 * (staged[3] - staged[4])
    padded = jnp.pad(me, ((1, 1), (0, 0)))
    along = 0.5 * (padded[2:] - padded[:-2])
    last = combine(me[None], first[None], second[None], along[None], a[None], b[None])[0]
    result = 0.5 * centre[0] + 0.5 * (me + TIME_STEP * last)
    return result.reshape(shape)


def split_parts(packed):
    flipped = jnp.swapaxes(packed, 1, 2)
    return jnp.stack([0.5 * (packed + flipped), 0.5 * (packed - flipped)])


def central(values, which_dim):
    padding = [(0, 0)] * values.ndim
    padding[which_dim] = (1, 1)
    padded = jnp.pad(values, padding)
    extent = values.shape[which_dim]
    return 0.5 * (
        lax.slice_in_dim(padded, 2, extent + 2, axis=which_dim)
        - lax.slice_in_dim(padded, 0, extent, axis=which_dim)
    )


def position_slopes(values):
    padded = padded_2(values, ((GX, 0),), 1)
    along_first = 0.5 * (padded[2:] - padded[:-2])
    return jnp.stack([along_first, central(values, 1), central(values, 2)])


def velocity_slopes(values):
    padded = extended(values, ((GX, 1), ("vert", 0)), 1)
    along_first = 0.5 * (padded[2:, 1:-1] - padded[:-2, 1:-1])
    along_second = 0.5 * (padded[1:-1, 2:] - padded[1:-1, :-2])
    return jnp.stack([along_first, along_second, central(values, 2)])


def coordinate(indices, cell_total):
    return (2.0 * indices.astype(jnp.float32) + 1.0 - cell_total) / cell_total


def velocity_grid(
    offset, slab_cells, first_count, second_offset, second_cells, second_count, third_count
):
    grid_shape = (slab_cells, second_cells, third_count)
    first_axis = coordinate(offset + jnp.arange(slab_cells, dtype=jnp.int32), first_count)
    second_axis = coordinate(
        second_offset + jnp.arange(second_cells, dtype=jnp.int32), second_count
    )
    third_axis = coordinate(jnp.arange(third_count, dtype=jnp.int32), third_count)
    return jnp.stack(
        [
            jnp.broadcast_to(first_axis[:, None, None], grid_shape),
            jnp.broadcast_to(second_axis[None, :, None], grid_shape),
            third_axis[None, None, :],
        ]
    )


def moments(factor, others, cells_count):
    return jnp.einsum("xyzr,dxyzs->drs", factor, others, precision=HIGHEST) / cells_count


def apply_pair(first_terms, first_mats, second_terms, second_mats):
    return -(
        jnp.einsum("dxyzs,drs->xyzr", first_terms, first_mats, precision=HIGHEST)
        + jnp.einsum("dxyzs,drs->xyzr", second_terms, second_mats, precision=HIGHEST)
    )


def newton_schulz(gram_matrix):
    frob_norm = jnp.sqrt(jnp.sum(gram_matrix * gram_matrix) + NORM_EPSILON)
    identity = jnp.eye(gram_matrix.shape[0], dtype=jnp.float32)
    root_part = gram_matrix / frob_norm
    inv_root = identity
    for sweep_index in range(NS_STEPS):
        middle = 1.5 * identity - 0.5 * jnp.dot(
            inv_root, root_part, precision=HIGHEST, preferred_element_type=jnp.float32
        )
        root_part = jnp.dot(
            root_part, middle, precision=HIGHEST, preferred_element_type=jnp.float32
        )
        inv_root = jnp.dot(middle, inv_root, precision=HIGHEST, preferred_element_type=jnp.float32)
    scale_root = jnp.sqrt(frob_norm)
    return (inv_root / scale_root, root_part * scale_root)


def sandwich(left_mats, core_matrix, right_mats):
    return jnp.einsum("dij,jk,dlk->il", left_mats, core_matrix, right_mats, precision=HIGHEST)


def per_device(position_factor, coefficients, velocity_factor, gravity):
    slab_vel = velocity_factor.shape[0]
    column_vel = velocity_factor.shape[1]
    first_count = slab_vel * lax.axis_size("vert")
    second_count = column_vel * lax.axis_size(GX)
    pos_cells = (
        position_factor.shape[0]
        * lax.axis_size(GX)
        * position_factor.shape[1]
        * position_factor.shape[2]
    )
    vel_cells = first_count * second_count * velocity_factor.shape[2]
    offset = lax.axis_index("vert") * slab_vel
    second_offset = lax.axis_index(GX) * column_vel
    velocity = velocity_grid(
        offset,
        slab_vel,
        first_count,
        second_offset,
        column_vel,
        second_count,
        velocity_factor.shape[2],
    )
    vel_first = moments(velocity_factor, velocity[..., None] * velocity_factor[None], vel_cells)
    stacked = slab_vel == 1 and column_vel == 1 and position_factor.shape[0] == 1
    around = {}
    if stacked:
        cells_p = position_factor.shape[1] * position_factor.shape[2]
        width = position_factor.shape[3]
        vel_rows = velocity_factor.reshape(-1, width)
        pos_rows = position_factor.reshape(cells_p, width)
        grav_flat = gravity.reshape(-1)
        grav_lines = -(-grav_flat.shape[0] // width)
        grav_rows = jnp.pad(grav_flat, (0, grav_lines * width - grav_flat.shape[0]))
        pos_pack = jnp.concatenate([pos_rows, grav_rows.reshape(grav_lines, width)])
        both = jnp.concatenate([vel_rows, pos_pack])
        got = {}
        for d in (1, -1, 2, -2):
            got[d] = from_behind(both, GX, -d)
        for d in (3, -3):
            got[d] = from_behind(pos_pack, GX, -d)
        for d in (4, -4):
            got[d] = from_behind(pos_rows, GX, -d)
        vc = vel_rows.shape[0]
        for d in (1, -1, 2, -2):
            around[(0, d)] = got[d][:vc]
            got[d] = got[d][vc:]
        lifted = jnp.stack([vel_rows, around[(0, 1)], around[(0, -1)]])
        for d in (1, -1):
            moved = from_behind(lifted, "vert", -d)
            around[(d, 0)], around[(d, 1)], around[(d, -1)] = moved[0], moved[1], moved[2]
        for d in (2, -2):
            around[(d, 0)] = from_behind(vel_rows, "vert", -d)
        around[(0, 0)] = vel_rows
        next_plane = around[(1, 0)].reshape(velocity_factor.shape)
        next_column = around[(0, 1)].reshape(velocity_factor.shape)
        plane_rows = [pos_rows if o == 0 else got[o][:cells_p] for o in range(-4, 5)]
        pos_planes = jnp.stack(plane_rows).reshape(9, *position_factor.shape[1:])
        grav_of = [grav_rows if o == 0 else got[o][cells_p:].reshape(-1) for o in range(-3, 4)]
        grav_planes = jnp.stack(
            [
                g[: grav_flat.shape[0]].reshape(gravity.shape[0], *position_factor.shape[1:3])
                for g in grav_of
            ]
        )
    else:
        next_plane = from_behind(velocity_factor, "vert", -1)
        next_column = from_behind(velocity_factor, GX, -1)
    following = jnp.concatenate([velocity_factor[1:], next_plane], axis=0)
    beside = jnp.concatenate([velocity_factor[:, 1:], next_column], axis=1)
    pair_sums = jnp.stack(
        [
            jnp.einsum("xyzr,xyzs->rs", velocity_factor, following, precision=HIGHEST),
            jnp.einsum("xyzr,xyzs->rs", velocity_factor, beside, precision=HIGHEST),
            jnp.einsum(
                "xyzr,xyzs->rs",
                velocity_factor[:, :, :-1],
                velocity_factor[:, :, 1:],
                precision=HIGHEST,
            ),
        ]
    )
    vel_second = 0.5 * (pair_sums - jnp.swapaxes(pair_sums, 1, 2)) / vel_cells
    vel_packed = (vel_first + vel_second).reshape(-1)
    vel_mats = split_parts(
        staged_total(vel_packed, ("gx_2", "gx_1", "vert", "gx_0")).reshape(vel_first.shape)
    )

    def position_rate(values):
        return apply_pair(
            position_slopes(values), vel_mats[0], gravity[..., None] * values[None], vel_mats[1]
        )

    if stacked:
        three = local_position_steps(pos_planes, grav_planes, coefficients, vel_mats)
        final_section = three[1:2]
        final_slopes = jnp.stack(
            [
                0.5 * (three[2:] - three[:-2]),
                central(final_section, 1),
                central(final_section, 2),
            ]
        )
    else:
        initial = jnp.einsum("xyzs,sr->xyzr", position_factor, coefficients, precision=HIGHEST)
        section_one = initial + TIME_STEP * position_rate(initial)
        section_two = 0.75 * initial + 0.25 * (section_one + TIME_STEP * position_rate(section_one))
        final_section = 1.0 / 3.0 * initial + 2.0 / 3.0 * (
            section_two + TIME_STEP * position_rate(section_two)
        )
        final_slopes = position_slopes(final_section)
    gram_part = (
        jnp.einsum("xyzr,xyzs->rs", final_section, final_section, precision=HIGHEST) / pos_cells
    )
    raw_terms = jnp.stack(
        [
            moments(final_section, final_slopes, pos_cells),
            moments(final_section, gravity[..., None] * final_section[None], pos_cells),
        ]
    )
    local_packed = jnp.concatenate([gram_part[None], raw_terms[0] + raw_terms[1]])
    packed = staged_total(local_packed.reshape(-1), ("gx_2", "gx_1", "gx_0")).reshape(
        local_packed.shape
    )
    gram_matrix = 0.5 * (packed[0] + packed[0].T)
    second_raw, first_raw = split_parts(packed[1:])
    summed_terms = jnp.stack([first_raw, second_raw])
    inv_root, root_part = newton_schulz(gram_matrix)
    new_position = jnp.einsum("xyzs,sr->xyzr", final_section, inv_root, precision=HIGHEST)
    pos_mats = jnp.einsum("ir,ndij,js->ndrs", inv_root, summed_terms, inv_root, precision=HIGHEST)
    coupled_core = root_part + TIME_STEP * (
        sandwich(pos_mats[0], root_part, vel_mats[0])
        + sandwich(pos_mats[1], root_part, vel_mats[1])
    )

    def velocity_rate(values):
        return apply_pair(
            velocity[..., None] * values[None], pos_mats[0], velocity_slopes(values), pos_mats[1]
        )

    if not stacked:
        vel_initial = jnp.einsum("abcs,rs->abcr", velocity_factor, coupled_core, precision=HIGHEST)
        vel_section = vel_initial + TIME_STEP * velocity_rate(vel_initial)
        new_velocity = 0.5 * vel_initial + 0.5 * (
            vel_section + TIME_STEP * velocity_rate(vel_section)
        )
        return (new_position, new_velocity)
    new_velocity = local_velocity_update(
        around, coupled_core, pos_mats, first_count, second_count, velocity_factor.shape
    )
    return (new_position, new_velocity)


def solution(mesh):
    finer = Mesh(
        mesh.devices.reshape(8, 4, 2, mesh.shape["vert"]), ("gx_0", "gx_1", "gx_2", "vert")
    )
    in_specs = (P(GX, None, None, None), P(), P("vert", GX, None, None), P(None, GX, None, None))
    out_specs = (P(GX, None, None, None), P("vert", GX, None, None))
    return jax.shard_map(
        per_device, mesh=finer, in_specs=in_specs, out_specs=out_specs, check_vma=False
    )
```

```python
import jax
import jax.numpy as jnp
from jax import lax
from jax.sharding import Mesh
from jax.sharding import PartitionSpec as P

NS_STEPS = 8
GX = ("gx_0", "gx_1", "gx_2")


HIGHEST = lax.Precision.HIGHEST
TIME_STEP = 0.25
NORM_EPSILON = 1e-06


def padded_2(block, sides, width):
    for axis, dim in sides:
        count = lax.axis_size(axis)
        forward = [(i, i + 1) for i in range(count - 1)]
        backward = [(target, source) for source, target in forward]
        low = lax.ppermute(
            lax.slice_in_dim(block, block.shape[dim] - width, None, axis=dim), axis, forward
        )
        high = lax.ppermute(lax.slice_in_dim(block, 0, width, axis=dim), axis, backward)
        block = jnp.concatenate([low, block, high], axis=dim)
    return block


def extended(value, sides, width):
    edges = {}
    for axis, dim in sides:
        devices, length = (lax.axis_size(axis), value.shape[dim])
        up = [(i, (i + 1) % devices) for i in range(devices - 1)]
        last = lax.slice_in_dim(value, length - width, length, axis=dim)
        first = lax.slice_in_dim(value, 0, width, axis=dim)
        edges[dim] = (
            lax.ppermute(last, axis, up),
            lax.ppermute(first, axis, [(b, a) for a, b in up]),
        )
    done = []
    for _, dim in sides:
        low, high = edges[dim]
        around = [(width, width) if d in done else (0, 0) for d in range(value.ndim)]
        value = jnp.concatenate([jnp.pad(low, around), value, jnp.pad(high, around)], axis=dim)
        done.append(dim)
    return value


def from_behind(block, axis, distance):
    devices = range(lax.axis_size(axis))
    route = [(i - distance, i) for i in devices if i - distance in devices]
    return lax.ppermute(block, axis, route)


def filled_up(lines, devices):
    spare = -len(lines) % devices
    return jnp.pad(lines, [(0, spare)] + [(0, 0)] * (lines.ndim - 1))


def from_everyone(value, axis):
    devices = lax.axis_size(axis)
    return lax.all_to_all(
        jnp.broadcast_to(value[None], (devices, *value.shape)), axis, 0, 0, tiled=True
    )


def laid_out(pieces, dim):
    dims = list(pieces.shape[1:])
    dims[dim] *= pieces.shape[0]
    return jnp.moveaxis(pieces, 0, dim).reshape(dims)


def whole_of(value, axes, dim):
    far, near = axes
    pieces = from_everyone(from_everyone(value, far), near)
    return laid_out(pieces.swapaxes(0, 1).reshape(-1, *value.shape), dim)


def split_up(value, dim, devices):
    dims = value.shape
    pieces = value.reshape(*dims[:dim], devices, dims[dim] // devices, *dims[dim + 1 :])
    return jnp.moveaxis(pieces, dim, 0)


def sum_at_owner(value, axis, dim):
    devices = lax.axis_size(axis)
    pieces = lax.all_to_all(split_up(value, dim, devices), axis, 0, 0, tiled=True)
    return jnp.sum(pieces, axis=0)


def sum_in_two_steps(value, axes, dim):
    far, near = axes
    own = sum_at_owner(split_up(value, dim, lax.axis_size(far)), near, dim + 1)
    return jnp.sum(lax.all_to_all(own, far, 0, 0, tiled=True), axis=0)


def total_of(value, axes):
    lines = value.reshape(-1, value.shape[-1])
    padded = filled_up(lines, lax.axis_size(axes[0]) * lax.axis_size(axes[1]))
    whole = whole_of(sum_in_two_steps(padded, axes, 0), axes, 0)
    return lax.slice_in_dim(whole, 0, len(lines)).reshape(value.shape)


def total_of_2(value, axes):
    own = sum_in_two_steps(
        filled_up(value, lax.axis_size(axes[0]) * lax.axis_size(axes[1])), axes, 0
    )
    whole = whole_of(own, axes, 0)
    return whole[: len(value)].reshape(value.shape)


def in_one(arrays, axis):
    flat, at, done = (jnp.concatenate([a.reshape(-1) for a in arrays]), 0, [])
    running = total_of_2(flat, axis)
    for a in arrays:
        done.append(running[at : at + a.size].reshape(a.shape))
        at += a.size
    return tuple(done)


def staged_total(flat, axes):
    sizes = [lax.axis_size(a) for a in axes]
    devices = 1
    for n in sizes:
        devices *= n
    length = flat.shape[0]
    piece = -(-length // (devices * 128)) * 128
    part = jnp.pad(flat, (0, piece * devices - length))
    for axis, n in zip(axes, sizes):
        rows = part.reshape(n, -1, 128)
        part = jnp.sum(lax.all_to_all(rows, axis, 0, 0, tiled=True), axis=0).reshape(-1)
    for axis, n in zip(axes[::-1], sizes[::-1]):
        rows = jnp.broadcast_to(part.reshape(1, -1, 128), (n, part.shape[0] // 128, 128))
        part = lax.all_to_all(rows, axis, 0, 0, tiled=True).reshape(-1)
    return part[:length]


CROSS = ((1, 0), (-1, 0), (0, 1), (0, -1))


def local_velocity_update(around, core, pos_mats, first_count, second_count, shape):
    a = lax.axis_index("vert")
    b = lax.axis_index(GX)
    offsets = list(around)
    blocks = jnp.stack([around[o].reshape(shape[2], shape[3]) for o in offsets])
    levels = jnp.einsum("nxs,rs->nxr", blocks, core, precision=HIGHEST)
    cells = shape[2]
    third = coordinate(jnp.arange(cells, dtype=jnp.int32), cells)[:, None]

    def combine(centre, first, second, along, first_pos, second_pos):
        terms = jnp.stack(
            [
                coordinate(first_pos, first_count)[..., None, None] * centre,
                coordinate(second_pos, second_count)[..., None, None] * centre,
                third * centre,
                first,
                second,
                along,
            ]
        )
        return -(
            jnp.einsum("dnxs,drs->nxr", terms[:3], pos_mats[0], precision=HIGHEST)
            + jnp.einsum("dnxs,drs->nxr", terms[3:], pos_mats[1], precision=HIGHEST)
        )

    inner = [(0, 0), *CROSS]
    index = {o: i for i, o in enumerate(offsets)}
    by_shift = {
        s: jnp.stack([levels[index[(o[0] + s[0], o[1] + s[1])]] for o in inner])
        for s in [(0, 0), *CROSS]
    }
    centre = by_shift[(0, 0)]
    first = 0.5 * (by_shift[(1, 0)] - by_shift[(-1, 0)])
    second = 0.5 * (by_shift[(0, 1)] - by_shift[(0, -1)])
    padded = jnp.pad(centre, ((0, 0), (1, 1), (0, 0)))
    along = 0.5 * (padded[:, 2:] - padded[:, :-2])
    rows = jnp.array([o[0] for o in inner]) + a
    cols = jnp.array([o[1] for o in inner]) + b
    inside = (rows >= 0) & (rows < first_count) & (cols >= 0) & (cols < second_count)
    staged = centre + TIME_STEP * combine(centre, first, second, along, rows, cols)
    staged = jnp.where(inside[:, None, None], staged, 0.0)
    me = staged[0]
    first = 0.5 * (staged[1] - staged[2])
    second = 0.5 * (staged[3] - staged[4])
    padded = jnp.pad(me, ((1, 1), (0, 0)))
    along = 0.5 * (padded[2:] - padded[:-2])
    last = combine(me[None], first[None], second[None], along[None], a[None], b[None])[0]
    result = 0.5 * centre[0] + 0.5 * (me + TIME_STEP * last)
    return result.reshape(shape)


def split_parts(packed):
    flipped = jnp.swapaxes(packed, 1, 2)
    return jnp.stack([0.5 * (packed + flipped), 0.5 * (packed - flipped)])


def central(values, which_dim):
    padding = [(0, 0)] * values.ndim
    padding[which_dim] = (1, 1)
    padded = jnp.pad(values, padding)
    extent = values.shape[which_dim]
    return 0.5 * (
        lax.slice_in_dim(padded, 2, extent + 2, axis=which_dim)
        - lax.slice_in_dim(padded, 0, extent, axis=which_dim)
    )


def slopes_carrying(values, to_next, to_previous):
    devices = lax.axis_size(GX)
    forward = [(i, i + 1) for i in range(devices - 1)]
    backward = [(target, source) for source, target in forward]
    width = values.shape[-1]
    rows = values.reshape(-1, width)
    cut = rows.shape[0]
    low = lax.ppermute(jnp.concatenate([rows, to_next.reshape(-1, width)]), GX, forward)
    high = lax.ppermute(jnp.concatenate([rows, to_previous.reshape(-1, width)]), GX, backward)
    along_first = 0.5 * (high[:cut] - low[:cut]).reshape(values.shape)
    slopes = jnp.stack([along_first, central(values, 1), central(values, 2)])
    return slopes, (low[cut:].reshape(to_next.shape), high[cut:].reshape(to_previous.shape))


def position_slopes(values):
    padded = padded_2(values, ((GX, 0),), 1)
    along_first = 0.5 * (padded[2:] - padded[:-2])
    return jnp.stack([along_first, central(values, 1), central(values, 2)])


def velocity_slopes(values):
    padded = extended(values, ((GX, 1), ("vert", 0)), 1)
    along_first = 0.5 * (padded[2:, 1:-1] - padded[:-2, 1:-1])
    along_second = 0.5 * (padded[1:-1, 2:] - padded[1:-1, :-2])
    return jnp.stack([along_first, along_second, central(values, 2)])


def coordinate(indices, cell_total):
    return (2.0 * indices.astype(jnp.float32) + 1.0 - cell_total) / cell_total


def velocity_grid(
    offset, slab_cells, first_count, second_offset, second_cells, second_count, third_count
):
    grid_shape = (slab_cells, second_cells, third_count)
    first_axis = coordinate(offset + jnp.arange(slab_cells, dtype=jnp.int32), first_count)
    second_axis = coordinate(
        second_offset + jnp.arange(second_cells, dtype=jnp.int32), second_count
    )
    third_axis = coordinate(jnp.arange(third_count, dtype=jnp.int32), third_count)
    return jnp.stack(
        [
            jnp.broadcast_to(first_axis[:, None, None], grid_shape),
            jnp.broadcast_to(second_axis[None, :, None], grid_shape),
            third_axis[None, None, :],
        ]
    )


def moments(factor, others, cells_count):
    return jnp.einsum("xyzr,dxyzs->drs", factor, others, precision=HIGHEST) / cells_count


def apply_pair(first_terms, first_mats, second_terms, second_mats):
    return -(
        jnp.einsum("dxyzs,drs->xyzr", first_terms, first_mats, precision=HIGHEST)
        + jnp.einsum("dxyzs,drs->xyzr", second_terms, second_mats, precision=HIGHEST)
    )


def newton_schulz(gram_matrix):
    frob_norm = jnp.sqrt(jnp.sum(gram_matrix * gram_matrix) + NORM_EPSILON)
    identity = jnp.eye(gram_matrix.shape[0], dtype=jnp.float32)
    root_part = gram_matrix / frob_norm
    inv_root = identity
    for sweep_index in range(NS_STEPS):
        middle = 1.5 * identity - 0.5 * jnp.dot(
            inv_root, root_part, precision=HIGHEST, preferred_element_type=jnp.float32
        )
        root_part = jnp.dot(
            root_part, middle, precision=HIGHEST, preferred_element_type=jnp.float32
        )
        inv_root = jnp.dot(middle, inv_root, precision=HIGHEST, preferred_element_type=jnp.float32)
    scale_root = jnp.sqrt(frob_norm)
    return (inv_root / scale_root, root_part * scale_root)


def sandwich(left_mats, core_matrix, right_mats):
    return jnp.einsum("dij,jk,dlk->il", left_mats, core_matrix, right_mats, precision=HIGHEST)


def per_device(position_factor, coefficients, velocity_factor, gravity):
    slab_vel = velocity_factor.shape[0]
    column_vel = velocity_factor.shape[1]
    first_count = slab_vel * lax.axis_size("vert")
    second_count = column_vel * lax.axis_size(GX)
    pos_cells = (
        position_factor.shape[0]
        * lax.axis_size(GX)
        * position_factor.shape[1]
        * position_factor.shape[2]
    )
    vel_cells = first_count * second_count * velocity_factor.shape[2]
    offset = lax.axis_index("vert") * slab_vel
    second_offset = lax.axis_index(GX) * column_vel
    velocity = velocity_grid(
        offset,
        slab_vel,
        first_count,
        second_offset,
        column_vel,
        second_count,
        velocity_factor.shape[2],
    )
    vel_first = moments(velocity_factor, velocity[..., None] * velocity_factor[None], vel_cells)
    next_plane = from_behind(velocity_factor, "vert", -1)
    next_column = from_behind(velocity_factor, GX, -1)
    around = {(1, 0): next_plane, (0, 1): next_column}
    riding = slab_vel == 1 and column_vel == 1 and position_factor.shape[0] == 1
    if riding:
        around[(-1, 0)] = from_behind(velocity_factor, "vert", 1)
        around[(0, 0)] = velocity_factor
    following = jnp.concatenate([velocity_factor[1:], next_plane], axis=0)
    beside = jnp.concatenate([velocity_factor[:, 1:], next_column], axis=1)
    pair_sums = jnp.stack(
        [
            jnp.einsum("xyzr,xyzs->rs", velocity_factor, following, precision=HIGHEST),
            jnp.einsum("xyzr,xyzs->rs", velocity_factor, beside, precision=HIGHEST),
            jnp.einsum(
                "xyzr,xyzs->rs",
                velocity_factor[:, :, :-1],
                velocity_factor[:, :, 1:],
                precision=HIGHEST,
            ),
        ]
    )
    vel_second = 0.5 * (pair_sums - jnp.swapaxes(pair_sums, 1, 2)) / vel_cells
    vel_packed = (vel_first + vel_second).reshape(-1)
    vel_mats = split_parts(
        staged_total(vel_packed, ("gx_2", "gx_1", "vert", "gx_0")).reshape(vel_first.shape)
    )

    def position_rate(values, slopes=None):
        if slopes is None:
            slopes = position_slopes(values)
        return apply_pair(slopes, vel_mats[0], gravity[..., None] * values[None], vel_mats[1])

    initial = jnp.einsum("xyzs,sr->xyzr", position_factor, coefficients, precision=HIGHEST)
    if riding:
        slopes, (behind, ahead) = slopes_carrying(initial, velocity_factor, velocity_factor)
        around[(0, -1)], around[(0, 1)] = behind, ahead
        lifted = (around[(0, 1)], around[(0, -1)])
        upper = from_behind(jnp.stack([around[(1, 0)], *lifted]), "vert", -1)
        lower = from_behind(jnp.stack([around[(-1, 0)], *lifted]), "vert", 1)
        around[(2, 0)], around[(1, 1)], around[(1, -1)] = upper[0], upper[1], upper[2]
        around[(-2, 0)], around[(-1, 1)], around[(-1, -1)] = lower[0], lower[1], lower[2]
        section_one = initial + TIME_STEP * position_rate(initial, slopes)
        slopes, (behind, ahead) = slopes_carrying(
            section_one, around[(0, -1)], around[(0, 1)]
        )
        around[(0, -2)], around[(0, 2)] = behind, ahead
        section_two = 0.75 * initial + 0.25 * (
            section_one + TIME_STEP * position_rate(section_one, slopes)
        )
    else:
        section_one = initial + TIME_STEP * position_rate(initial)
        section_two = 0.75 * initial + 0.25 * (
            section_one + TIME_STEP * position_rate(section_one)
        )
    final_section = 1.0 / 3.0 * initial + 2.0 / 3.0 * (
        section_two + TIME_STEP * position_rate(section_two)
    )
    gram_part = (
        jnp.einsum("xyzr,xyzs->rs", final_section, final_section, precision=HIGHEST) / pos_cells
    )
    raw_terms = jnp.stack(
        [
            moments(final_section, position_slopes(final_section), pos_cells),
            moments(final_section, gravity[..., None] * final_section[None], pos_cells),
        ]
    )
    local_packed = jnp.concatenate([gram_part[None], raw_terms[0] + raw_terms[1]])
    packed = staged_total(local_packed.reshape(-1), ("gx_2", "gx_1", "gx_0")).reshape(
        local_packed.shape
    )
    gram_matrix = 0.5 * (packed[0] + packed[0].T)
    second_raw, first_raw = split_parts(packed[1:])
    summed_terms = jnp.stack([first_raw, second_raw])
    inv_root, root_part = newton_schulz(gram_matrix)
    new_position = jnp.einsum("xyzs,sr->xyzr", final_section, inv_root, precision=HIGHEST)
    pos_mats = jnp.einsum("ir,ndij,js->ndrs", inv_root, summed_terms, inv_root, precision=HIGHEST)
    coupled_core = root_part + TIME_STEP * (
        sandwich(pos_mats[0], root_part, vel_mats[0])
        + sandwich(pos_mats[1], root_part, vel_mats[1])
    )

    def velocity_rate(values):
        return apply_pair(
            velocity[..., None] * values[None], pos_mats[0], velocity_slopes(values), pos_mats[1]
        )

    if not riding:
        vel_initial = jnp.einsum("abcs,rs->abcr", velocity_factor, coupled_core, precision=HIGHEST)
        vel_section = vel_initial + TIME_STEP * velocity_rate(vel_initial)
        new_velocity = 0.5 * vel_initial + 0.5 * (
            vel_section + TIME_STEP * velocity_rate(vel_section)
        )
        return (new_position, new_velocity)
    new_velocity = local_velocity_update(
        around, coupled_core, pos_mats, first_count, second_count, velocity_factor.shape
    )
    return (new_position, new_velocity)


def solution(mesh):
    finer = Mesh(
        mesh.devices.reshape(8, 4, 2, mesh.shape["vert"]), ("gx_0", "gx_1", "gx_2", "vert")
    )
    in_specs = (P(GX, None, None, None), P(), P("vert", GX, None, None), P(None, GX, None, None))
    out_specs = (P(GX, None, None, None), P("vert", GX, None, None))
    return jax.shard_map(
        per_device, mesh=finer, in_specs=in_specs, out_specs=out_specs, check_vma=False
    )
```

```python
import jax
import jax.numpy as jnp
from jax import lax
from jax.sharding import Mesh
from jax.sharding import PartitionSpec as P

NS_STEPS = 8
GX = ("gx_0", "gx_1", "gx_2")


HIGHEST = lax.Precision.HIGHEST
TIME_STEP = 0.25
NORM_EPSILON = 1e-06


def padded_2(block, sides, width):
    for axis, dim in sides:
        count = lax.axis_size(axis)
        forward = [(i, i + 1) for i in range(count - 1)]
        backward = [(target, source) for source, target in forward]
        low = lax.ppermute(
            lax.slice_in_dim(block, block.shape[dim] - width, None, axis=dim), axis, forward
        )
        high = lax.ppermute(lax.slice_in_dim(block, 0, width, axis=dim), axis, backward)
        block = jnp.concatenate([low, block, high], axis=dim)
    return block


def extended(value, sides, width):
    edges = {}
    for axis, dim in sides:
        devices, length = (lax.axis_size(axis), value.shape[dim])
        up = [(i, (i + 1) % devices) for i in range(devices - 1)]
        last = lax.slice_in_dim(value, length - width, length, axis=dim)
        first = lax.slice_in_dim(value, 0, width, axis=dim)
        edges[dim] = (
            lax.ppermute(last, axis, up),
            lax.ppermute(first, axis, [(b, a) for a, b in up]),
        )
    done = []
    for _, dim in sides:
        low, high = edges[dim]
        around = [(width, width) if d in done else (0, 0) for d in range(value.ndim)]
        value = jnp.concatenate([jnp.pad(low, around), value, jnp.pad(high, around)], axis=dim)
        done.append(dim)
    return value


def from_behind(block, axis, distance):
    devices = range(lax.axis_size(axis))
    route = [(i - distance, i) for i in devices if i - distance in devices]
    return lax.ppermute(block, axis, route)


def filled_up(lines, devices):
    spare = -len(lines) % devices
    return jnp.pad(lines, [(0, spare)] + [(0, 0)] * (lines.ndim - 1))


def from_everyone(value, axis):
    devices = lax.axis_size(axis)
    return lax.all_to_all(
        jnp.broadcast_to(value[None], (devices, *value.shape)), axis, 0, 0, tiled=True
    )


def laid_out(pieces, dim):
    dims = list(pieces.shape[1:])
    dims[dim] *= pieces.shape[0]
    return jnp.moveaxis(pieces, 0, dim).reshape(dims)


def whole_of(value, axes, dim):
    far, near = axes
    pieces = from_everyone(from_everyone(value, far), near)
    return laid_out(pieces.swapaxes(0, 1).reshape(-1, *value.shape), dim)


def split_up(value, dim, devices):
    dims = value.shape
    pieces = value.reshape(*dims[:dim], devices, dims[dim] // devices, *dims[dim + 1 :])
    return jnp.moveaxis(pieces, dim, 0)


def sum_at_owner(value, axis, dim):
    devices = lax.axis_size(axis)
    pieces = lax.all_to_all(split_up(value, dim, devices), axis, 0, 0, tiled=True)
    return jnp.sum(pieces, axis=0)


def sum_in_two_steps(value, axes, dim):
    far, near = axes
    own = sum_at_owner(split_up(value, dim, lax.axis_size(far)), near, dim + 1)
    return jnp.sum(lax.all_to_all(own, far, 0, 0, tiled=True), axis=0)


def total_of(value, axes):
    lines = value.reshape(-1, value.shape[-1])
    padded = filled_up(lines, lax.axis_size(axes[0]) * lax.axis_size(axes[1]))
    whole = whole_of(sum_in_two_steps(padded, axes, 0), axes, 0)
    return lax.slice_in_dim(whole, 0, len(lines)).reshape(value.shape)


def total_of_2(value, axes):
    own = sum_in_two_steps(
        filled_up(value, lax.axis_size(axes[0]) * lax.axis_size(axes[1])), axes, 0
    )
    whole = whole_of(own, axes, 0)
    return whole[: len(value)].reshape(value.shape)


def in_one(arrays, axis):
    flat, at, done = (jnp.concatenate([a.reshape(-1) for a in arrays]), 0, [])
    running = total_of_2(flat, axis)
    for a in arrays:
        done.append(running[at : at + a.size].reshape(a.shape))
        at += a.size
    return tuple(done)


def staged_total(flat, axes):
    sizes = [lax.axis_size(a) for a in axes]
    devices = 1
    for n in sizes:
        devices *= n
    length = flat.shape[0]
    piece = -(-length // (devices * 128)) * 128
    part = jnp.pad(flat, (0, piece * devices - length))
    for axis, n in zip(axes, sizes):
        rows = part.reshape(n, -1, 128)
        part = jnp.sum(lax.all_to_all(rows, axis, 0, 0, tiled=True), axis=0).reshape(-1)
    for axis, n in zip(axes[::-1], sizes[::-1]):
        rows = jnp.broadcast_to(part.reshape(1, -1, 128), (n, part.shape[0] // 128, 128))
        part = lax.all_to_all(rows, axis, 0, 0, tiled=True).reshape(-1)
    return part[:length]


def split_parts(packed):
    flipped = jnp.swapaxes(packed, 1, 2)
    return jnp.stack([0.5 * (packed + flipped), 0.5 * (packed - flipped)])


def central(values, which_dim):
    padding = [(0, 0)] * values.ndim
    padding[which_dim] = (1, 1)
    padded = jnp.pad(values, padding)
    extent = values.shape[which_dim]
    return 0.5 * (
        lax.slice_in_dim(padded, 2, extent + 2, axis=which_dim)
        - lax.slice_in_dim(padded, 0, extent, axis=which_dim)
    )


def position_slopes(values):
    padded = padded_2(values, ((GX, 0),), 1)
    along_first = 0.5 * (padded[2:] - padded[:-2])
    return jnp.stack([along_first, central(values, 1), central(values, 2)])


def velocity_slopes(values):
    padded = extended(values, ((GX, 1), ("vert", 0)), 1)
    along_first = 0.5 * (padded[2:, 1:-1] - padded[:-2, 1:-1])
    along_second = 0.5 * (padded[1:-1, 2:] - padded[1:-1, :-2])
    return jnp.stack([along_first, along_second, central(values, 2)])


def coordinate(indices, cell_total):
    return (2.0 * indices.astype(jnp.float32) + 1.0 - cell_total) / cell_total


def velocity_grid(
    offset, slab_cells, first_count, second_offset, second_cells, second_count, third_count
):
    grid_shape = (slab_cells, second_cells, third_count)
    first_axis = coordinate(offset + jnp.arange(slab_cells, dtype=jnp.int32), first_count)
    second_axis = coordinate(
        second_offset + jnp.arange(second_cells, dtype=jnp.int32), second_count
    )
    third_axis = coordinate(jnp.arange(third_count, dtype=jnp.int32), third_count)
    return jnp.stack(
        [
            jnp.broadcast_to(first_axis[:, None, None], grid_shape),
            jnp.broadcast_to(second_axis[None, :, None], grid_shape),
            third_axis[None, None, :],
        ]
    )


def moments(factor, others, cells_count):
    return jnp.einsum("xyzr,dxyzs->drs", factor, others, precision=HIGHEST) / cells_count


def apply_pair(first_terms, first_mats, second_terms, second_mats):
    return -(
        jnp.einsum("dxyzs,drs->xyzr", first_terms, first_mats, precision=HIGHEST)
        + jnp.einsum("dxyzs,drs->xyzr", second_terms, second_mats, precision=HIGHEST)
    )


def newton_schulz(gram_matrix):
    frob_norm = jnp.sqrt(jnp.sum(gram_matrix * gram_matrix) + NORM_EPSILON)
    identity = jnp.eye(gram_matrix.shape[0], dtype=jnp.float32)
    root_part = gram_matrix / frob_norm
    inv_root = identity
    for sweep_index in range(NS_STEPS):
        middle = 1.5 * identity - 0.5 * jnp.dot(
            inv_root, root_part, precision=HIGHEST, preferred_element_type=jnp.float32
        )
        root_part = jnp.dot(
            root_part, middle, precision=HIGHEST, preferred_element_type=jnp.float32
        )
        inv_root = jnp.dot(middle, inv_root, precision=HIGHEST, preferred_element_type=jnp.float32)
    scale_root = jnp.sqrt(frob_norm)
    return (inv_root / scale_root, root_part * scale_root)


def sandwich(left_mats, core_matrix, right_mats):
    return jnp.einsum("dij,jk,dlk->il", left_mats, core_matrix, right_mats, precision=HIGHEST)


def per_device(position_factor, coefficients, velocity_factor, gravity):
    slab_vel = velocity_factor.shape[0]
    column_vel = velocity_factor.shape[1]
    first_count = slab_vel * lax.axis_size("vert")
    second_count = column_vel * lax.axis_size(GX)
    pos_cells = (
        position_factor.shape[0]
        * lax.axis_size(GX)
        * position_factor.shape[1]
        * position_factor.shape[2]
    )
    vel_cells = first_count * second_count * velocity_factor.shape[2]
    offset = lax.axis_index("vert") * slab_vel
    second_offset = lax.axis_index(GX) * column_vel
    velocity = velocity_grid(
        offset,
        slab_vel,
        first_count,
        second_offset,
        column_vel,
        second_count,
        velocity_factor.shape[2],
    )
    vel_first = moments(velocity_factor, velocity[..., None] * velocity_factor[None], vel_cells)
    next_plane = from_behind(velocity_factor, "vert", -1)
    next_column = from_behind(velocity_factor, GX, -1)
    following = jnp.concatenate([velocity_factor[1:], next_plane], axis=0)
    beside = jnp.concatenate([velocity_factor[:, 1:], next_column], axis=1)
    pair_sums = jnp.stack(
        [
            jnp.einsum("xyzr,xyzs->rs", velocity_factor, following, precision=HIGHEST),
            jnp.einsum("xyzr,xyzs->rs", velocity_factor, beside, precision=HIGHEST),
            jnp.einsum(
                "xyzr,xyzs->rs",
                velocity_factor[:, :, :-1],
                velocity_factor[:, :, 1:],
                precision=HIGHEST,
            ),
        ]
    )
    vel_second = 0.5 * (pair_sums - jnp.swapaxes(pair_sums, 1, 2)) / vel_cells
    vel_packed = (vel_first + vel_second).reshape(-1)
    vel_mats = split_parts(
        staged_total(vel_packed, (("gx_1", "gx_2"), "vert", "gx_0")).reshape(vel_first.shape)
    )

    def position_rate(values):
        return apply_pair(
            position_slopes(values), vel_mats[0], gravity[..., None] * values[None], vel_mats[1]
        )

    initial = jnp.einsum("xyzs,sr->xyzr", position_factor, coefficients, precision=HIGHEST)
    section_one = initial + TIME_STEP * position_rate(initial)
    section_two = 0.75 * initial + 0.25 * (section_one + TIME_STEP * position_rate(section_one))
    final_section = 1.0 / 3.0 * initial + 2.0 / 3.0 * (
        section_two + TIME_STEP * position_rate(section_two)
    )
    gram_part = (
        jnp.einsum("xyzr,xyzs->rs", final_section, final_section, precision=HIGHEST) / pos_cells
    )
    raw_terms = jnp.stack(
        [
            moments(final_section, position_slopes(final_section), pos_cells),
            moments(final_section, gravity[..., None] * final_section[None], pos_cells),
        ]
    )
    local_packed = jnp.concatenate([gram_part[None], raw_terms[0] + raw_terms[1]])
    packed = staged_total(local_packed.reshape(-1), (("gx_1", "gx_2"), "gx_0")).reshape(
        local_packed.shape
    )
    gram_matrix = 0.5 * (packed[0] + packed[0].T)
    second_raw, first_raw = split_parts(packed[1:])
    summed_terms = jnp.stack([first_raw, second_raw])
    inv_root, root_part = newton_schulz(gram_matrix)
    new_position = jnp.einsum("xyzs,sr->xyzr", final_section, inv_root, precision=HIGHEST)
    pos_mats = jnp.einsum("ir,ndij,js->ndrs", inv_root, summed_terms, inv_root, precision=HIGHEST)
    coupled_core = root_part + TIME_STEP * (
        sandwich(pos_mats[0], root_part, vel_mats[0])
        + sandwich(pos_mats[1], root_part, vel_mats[1])
    )

    def velocity_rate(values):
        return apply_pair(
            velocity[..., None] * values[None], pos_mats[0], velocity_slopes(values), pos_mats[1]
        )

    vel_initial = jnp.einsum("abcs,rs->abcr", velocity_factor, coupled_core, precision=HIGHEST)
    vel_section = vel_initial + TIME_STEP * velocity_rate(vel_initial)
    new_velocity = 0.5 * vel_initial + 0.5 * (vel_section + TIME_STEP * velocity_rate(vel_section))
    return (new_position, new_velocity)


def solution(mesh):
    finer = Mesh(
        mesh.devices.reshape(8, 4, 2, mesh.shape["vert"]), ("gx_0", "gx_1", "gx_2", "vert")
    )
    in_specs = (P(GX, None, None, None), P(), P("vert", GX, None, None), P(None, GX, None, None))
    out_specs = (P(GX, None, None, None), P("vert", GX, None, None))
    return jax.shard_map(
        per_device, mesh=finer, in_specs=in_specs, out_specs=out_specs, check_vma=False
    )
```

```python
import jax
import jax.numpy as jnp
from jax import lax
from jax.sharding import Mesh
from jax.sharding import PartitionSpec as P

NS_STEPS = 8
GX = ("gx_0", "gx_1", "gx_2")


HIGHEST = lax.Precision.HIGHEST
TIME_STEP = 0.25
NORM_EPSILON = 1e-06


def padded_2(block, sides, width):
    for axis, dim in sides:
        count = lax.axis_size(axis)
        forward = [(i, i + 1) for i in range(count - 1)]
        backward = [(target, source) for source, target in forward]
        low = lax.ppermute(
            lax.slice_in_dim(block, block.shape[dim] - width, None, axis=dim), axis, forward
        )
        high = lax.ppermute(lax.slice_in_dim(block, 0, width, axis=dim), axis, backward)
        block = jnp.concatenate([low, block, high], axis=dim)
    return block


def extended(value, sides, width):
    edges = {}
    for axis, dim in sides:
        devices, length = (lax.axis_size(axis), value.shape[dim])
        up = [(i, (i + 1) % devices) for i in range(devices - 1)]
        last = lax.slice_in_dim(value, length - width, length, axis=dim)
        first = lax.slice_in_dim(value, 0, width, axis=dim)
        edges[dim] = (
            lax.ppermute(last, axis, up),
            lax.ppermute(first, axis, [(b, a) for a, b in up]),
        )
    done = []
    for _, dim in sides:
        low, high = edges[dim]
        around = [(width, width) if d in done else (0, 0) for d in range(value.ndim)]
        value = jnp.concatenate([jnp.pad(low, around), value, jnp.pad(high, around)], axis=dim)
        done.append(dim)
    return value


def from_behind(block, axis, distance):
    devices = range(lax.axis_size(axis))
    route = [(i - distance, i) for i in devices if i - distance in devices]
    return lax.ppermute(block, axis, route)


def filled_up(lines, devices):
    spare = -len(lines) % devices
    return jnp.pad(lines, [(0, spare)] + [(0, 0)] * (lines.ndim - 1))


def from_everyone(value, axis):
    devices = lax.axis_size(axis)
    return lax.all_to_all(
        jnp.broadcast_to(value[None], (devices, *value.shape)), axis, 0, 0, tiled=True
    )


def laid_out(pieces, dim):
    dims = list(pieces.shape[1:])
    dims[dim] *= pieces.shape[0]
    return jnp.moveaxis(pieces, 0, dim).reshape(dims)


def whole_of(value, axes, dim):
    far, near = axes
    pieces = from_everyone(from_everyone(value, far), near)
    return laid_out(pieces.swapaxes(0, 1).reshape(-1, *value.shape), dim)


def split_up(value, dim, devices):
    dims = value.shape
    pieces = value.reshape(*dims[:dim], devices, dims[dim] // devices, *dims[dim + 1 :])
    return jnp.moveaxis(pieces, dim, 0)


def sum_at_owner(value, axis, dim):
    devices = lax.axis_size(axis)
    pieces = lax.all_to_all(split_up(value, dim, devices), axis, 0, 0, tiled=True)
    return jnp.sum(pieces, axis=0)


def sum_in_two_steps(value, axes, dim):
    far, near = axes
    own = sum_at_owner(split_up(value, dim, lax.axis_size(far)), near, dim + 1)
    return jnp.sum(lax.all_to_all(own, far, 0, 0, tiled=True), axis=0)


def total_of(value, axes):
    lines = value.reshape(-1, value.shape[-1])
    padded = filled_up(lines, lax.axis_size(axes[0]) * lax.axis_size(axes[1]))
    whole = whole_of(sum_in_two_steps(padded, axes, 0), axes, 0)
    return lax.slice_in_dim(whole, 0, len(lines)).reshape(value.shape)


def total_of_2(value, axes):
    own = sum_in_two_steps(
        filled_up(value, lax.axis_size(axes[0]) * lax.axis_size(axes[1])), axes, 0
    )
    whole = whole_of(own, axes, 0)
    return whole[: len(value)].reshape(value.shape)


def in_one(arrays, axis):
    flat, at, done = (jnp.concatenate([a.reshape(-1) for a in arrays]), 0, [])
    running = total_of_2(flat, axis)
    for a in arrays:
        done.append(running[at : at + a.size].reshape(a.shape))
        at += a.size
    return tuple(done)


def doubled_total(part, axis, n):
    if n & (n - 1):
        return lax.psum(part, axis)
    step = 1
    while step < n:
        pairs = [(i, i ^ step) for i in range(n)]
        part = part + lax.ppermute(part, axis, pairs)
        step *= 2
    return part


def staged_total(flat, axes):
    sizes = [lax.axis_size(a) for a in axes]
    devices = 1
    for n in sizes:
        devices *= n
    length = flat.shape[0]
    piece = -(-length // (devices // sizes[-1] * 128)) * 128
    devices = devices // sizes[-1]
    part = jnp.pad(flat, (0, piece * devices - length))
    for axis, n in zip(axes[:-1], sizes[:-1]):
        rows = part.reshape(n, -1, 128)
        part = jnp.sum(lax.all_to_all(rows, axis, 0, 0, tiled=True), axis=0).reshape(-1)
    part = doubled_total(part, axes[-1], sizes[-1])
    for axis, n in zip(axes[-2::-1], sizes[-2::-1]):
        rows = jnp.broadcast_to(part.reshape(1, -1, 128), (n, part.shape[0] // 128, 128))
        part = lax.all_to_all(rows, axis, 0, 0, tiled=True).reshape(-1)
    return part[:length]


def split_parts(packed):
    flipped = jnp.swapaxes(packed, 1, 2)
    return jnp.stack([0.5 * (packed + flipped), 0.5 * (packed - flipped)])


def central(values, which_dim):
    padding = [(0, 0)] * values.ndim
    padding[which_dim] = (1, 1)
    padded = jnp.pad(values, padding)
    extent = values.shape[which_dim]
    return 0.5 * (
        lax.slice_in_dim(padded, 2, extent + 2, axis=which_dim)
        - lax.slice_in_dim(padded, 0, extent, axis=which_dim)
    )


def position_slopes(values):
    padded = padded_2(values, ((GX, 0),), 1)
    along_first = 0.5 * (padded[2:] - padded[:-2])
    return jnp.stack([along_first, central(values, 1), central(values, 2)])


def velocity_slopes(values):
    padded = extended(values, ((GX, 1), ("vert", 0)), 1)
    along_first = 0.5 * (padded[2:, 1:-1] - padded[:-2, 1:-1])
    along_second = 0.5 * (padded[1:-1, 2:] - padded[1:-1, :-2])
    return jnp.stack([along_first, along_second, central(values, 2)])


def coordinate(indices, cell_total):
    return (2.0 * indices.astype(jnp.float32) + 1.0 - cell_total) / cell_total


def velocity_grid(
    offset, slab_cells, first_count, second_offset, second_cells, second_count, third_count
):
    grid_shape = (slab_cells, second_cells, third_count)
    first_axis = coordinate(offset + jnp.arange(slab_cells, dtype=jnp.int32), first_count)
    second_axis = coordinate(
        second_offset + jnp.arange(second_cells, dtype=jnp.int32), second_count
    )
    third_axis = coordinate(jnp.arange(third_count, dtype=jnp.int32), third_count)
    return jnp.stack(
        [
            jnp.broadcast_to(first_axis[:, None, None], grid_shape),
            jnp.broadcast_to(second_axis[None, :, None], grid_shape),
            third_axis[None, None, :],
        ]
    )


def moments(factor, others, cells_count):
    return jnp.einsum("xyzr,dxyzs->drs", factor, others, precision=HIGHEST) / cells_count


def apply_pair(first_terms, first_mats, second_terms, second_mats):
    return -(
        jnp.einsum("dxyzs,drs->xyzr", first_terms, first_mats, precision=HIGHEST)
        + jnp.einsum("dxyzs,drs->xyzr", second_terms, second_mats, precision=HIGHEST)
    )


def newton_schulz(gram_matrix):
    frob_norm = jnp.sqrt(jnp.sum(gram_matrix * gram_matrix) + NORM_EPSILON)
    identity = jnp.eye(gram_matrix.shape[0], dtype=jnp.float32)
    root_part = gram_matrix / frob_norm
    inv_root = identity
    for sweep_index in range(NS_STEPS):
        middle = 1.5 * identity - 0.5 * jnp.dot(
            inv_root, root_part, precision=HIGHEST, preferred_element_type=jnp.float32
        )
        root_part = jnp.dot(
            root_part, middle, precision=HIGHEST, preferred_element_type=jnp.float32
        )
        inv_root = jnp.dot(middle, inv_root, precision=HIGHEST, preferred_element_type=jnp.float32)
    scale_root = jnp.sqrt(frob_norm)
    return (inv_root / scale_root, root_part * scale_root)


def sandwich(left_mats, core_matrix, right_mats):
    return jnp.einsum("dij,jk,dlk->il", left_mats, core_matrix, right_mats, precision=HIGHEST)


def per_device(position_factor, coefficients, velocity_factor, gravity):
    slab_vel = velocity_factor.shape[0]
    column_vel = velocity_factor.shape[1]
    first_count = slab_vel * lax.axis_size("vert")
    second_count = column_vel * lax.axis_size(GX)
    pos_cells = (
        position_factor.shape[0]
        * lax.axis_size(GX)
        * position_factor.shape[1]
        * position_factor.shape[2]
    )
    vel_cells = first_count * second_count * velocity_factor.shape[2]
    offset = lax.axis_index("vert") * slab_vel
    second_offset = lax.axis_index(GX) * column_vel
    velocity = velocity_grid(
        offset,
        slab_vel,
        first_count,
        second_offset,
        column_vel,
        second_count,
        velocity_factor.shape[2],
    )
    vel_first = moments(velocity_factor, velocity[..., None] * velocity_factor[None], vel_cells)
    next_plane = from_behind(velocity_factor, "vert", -1)
    next_column = from_behind(velocity_factor, GX, -1)
    following = jnp.concatenate([velocity_factor[1:], next_plane], axis=0)
    beside = jnp.concatenate([velocity_factor[:, 1:], next_column], axis=1)
    pair_sums = jnp.stack(
        [
            jnp.einsum("xyzr,xyzs->rs", velocity_factor, following, precision=HIGHEST),
            jnp.einsum("xyzr,xyzs->rs", velocity_factor, beside, precision=HIGHEST),
            jnp.einsum(
                "xyzr,xyzs->rs",
                velocity_factor[:, :, :-1],
                velocity_factor[:, :, 1:],
                precision=HIGHEST,
            ),
        ]
    )
    vel_second = 0.5 * (pair_sums - jnp.swapaxes(pair_sums, 1, 2)) / vel_cells
    vel_packed = (vel_first + vel_second).reshape(-1)
    vel_mats = split_parts(
        staged_total(vel_packed, (("gx_1", "gx_2"), "vert", "gx_0")).reshape(vel_first.shape)
    )

    def position_rate(values):
        return apply_pair(
            position_slopes(values), vel_mats[0], gravity[..., None] * values[None], vel_mats[1]
        )

    initial = jnp.einsum("xyzs,sr->xyzr", position_factor, coefficients, precision=HIGHEST)
    section_one = initial + TIME_STEP * position_rate(initial)
    section_two = 0.75 * initial + 0.25 * (section_one + TIME_STEP * position_rate(section_one))
    final_section = 1.0 / 3.0 * initial + 2.0 / 3.0 * (
        section_two + TIME_STEP * position_rate(section_two)
    )
    gram_part = (
        jnp.einsum("xyzr,xyzs->rs", final_section, final_section, precision=HIGHEST) / pos_cells
    )
    raw_terms = jnp.stack(
        [
            moments(final_section, position_slopes(final_section), pos_cells),
            moments(final_section, gravity[..., None] * final_section[None], pos_cells),
        ]
    )
    local_packed = jnp.concatenate([gram_part[None], raw_terms[0] + raw_terms[1]])
    packed = staged_total(local_packed.reshape(-1), (("gx_1", "gx_2"), "gx_0")).reshape(
        local_packed.shape
    )
    gram_matrix = 0.5 * (packed[0] + packed[0].T)
    second_raw, first_raw = split_parts(packed[1:])
    summed_terms = jnp.stack([first_raw, second_raw])
    inv_root, root_part = newton_schulz(gram_matrix)
    new_position = jnp.einsum("xyzs,sr->xyzr", final_section, inv_root, precision=HIGHEST)
    pos_mats = jnp.einsum("ir,ndij,js->ndrs", inv_root, summed_terms, inv_root, precision=HIGHEST)
    coupled_core = root_part + TIME_STEP * (
        sandwich(pos_mats[0], root_part, vel_mats[0])
        + sandwich(pos_mats[1], root_part, vel_mats[1])
    )

    def velocity_rate(values):
        return apply_pair(
            velocity[..., None] * values[None], pos_mats[0], velocity_slopes(values), pos_mats[1]
        )

    vel_initial = jnp.einsum("abcs,rs->abcr", velocity_factor, coupled_core, precision=HIGHEST)
    vel_section = vel_initial + TIME_STEP * velocity_rate(vel_initial)
    new_velocity = 0.5 * vel_initial + 0.5 * (vel_section + TIME_STEP * velocity_rate(vel_section))
    return (new_position, new_velocity)


def solution(mesh):
    finer = Mesh(
        mesh.devices.reshape(8, 4, 2, mesh.shape["vert"]), ("gx_0", "gx_1", "gx_2", "vert")
    )
    in_specs = (P(GX, None, None, None), P(), P("vert", GX, None, None), P(None, GX, None, None))
    out_specs = (P(GX, None, None, None), P("vert", GX, None, None))
    return jax.shard_map(
        per_device, mesh=finer, in_specs=in_specs, out_specs=out_specs, check_vma=False
    )
```

```python
import jax
import jax.numpy as jnp
from jax import lax
from jax.sharding import Mesh
from jax.sharding import PartitionSpec as P

NS_STEPS = 8
GX = ("gx_0", "gx_1", "gx_2")


HIGHEST = lax.Precision.HIGHEST
TIME_STEP = 0.25
NORM_EPSILON = 1e-06


def padded_2(block, sides, width):
    for axis, dim in sides:
        count = lax.axis_size(axis)
        forward = [(i, i + 1) for i in range(count - 1)]
        backward = [(target, source) for source, target in forward]
        low = lax.ppermute(
            lax.slice_in_dim(block, block.shape[dim] - width, None, axis=dim), axis, forward
        )
        high = lax.ppermute(lax.slice_in_dim(block, 0, width, axis=dim), axis, backward)
        block = jnp.concatenate([low, block, high], axis=dim)
    return block


def extended(value, sides, width):
    edges = {}
    for axis, dim in sides:
        devices, length = (lax.axis_size(axis), value.shape[dim])
        up = [(i, (i + 1) % devices) for i in range(devices - 1)]
        last = lax.slice_in_dim(value, length - width, length, axis=dim)
        first = lax.slice_in_dim(value, 0, width, axis=dim)
        edges[dim] = (
            lax.ppermute(last, axis, up),
            lax.ppermute(first, axis, [(b, a) for a, b in up]),
        )
    done = []
    for _, dim in sides:
        low, high = edges[dim]
        around = [(width, width) if d in done else (0, 0) for d in range(value.ndim)]
        value = jnp.concatenate([jnp.pad(low, around), value, jnp.pad(high, around)], axis=dim)
        done.append(dim)
    return value


def from_behind(block, axis, distance):
    devices = range(lax.axis_size(axis))
    route = [(i - distance, i) for i in devices if i - distance in devices]
    return lax.ppermute(block, axis, route)


def filled_up(lines, devices):
    spare = -len(lines) % devices
    return jnp.pad(lines, [(0, spare)] + [(0, 0)] * (lines.ndim - 1))


def from_everyone(value, axis):
    devices = lax.axis_size(axis)
    return lax.all_to_all(
        jnp.broadcast_to(value[None], (devices, *value.shape)), axis, 0, 0, tiled=True
    )


def laid_out(pieces, dim):
    dims = list(pieces.shape[1:])
    dims[dim] *= pieces.shape[0]
    return jnp.moveaxis(pieces, 0, dim).reshape(dims)


def whole_of(value, axes, dim):
    far, near = axes
    pieces = from_everyone(from_everyone(value, far), near)
    return laid_out(pieces.swapaxes(0, 1).reshape(-1, *value.shape), dim)


def split_up(value, dim, devices):
    dims = value.shape
    pieces = value.reshape(*dims[:dim], devices, dims[dim] // devices, *dims[dim + 1 :])
    return jnp.moveaxis(pieces, dim, 0)


def sum_at_owner(value, axis, dim):
    devices = lax.axis_size(axis)
    pieces = lax.all_to_all(split_up(value, dim, devices), axis, 0, 0, tiled=True)
    return jnp.sum(pieces, axis=0)


def sum_in_two_steps(value, axes, dim):
    far, near = axes
    own = sum_at_owner(split_up(value, dim, lax.axis_size(far)), near, dim + 1)
    return jnp.sum(lax.all_to_all(own, far, 0, 0, tiled=True), axis=0)


def total_of(value, axes):
    lines = value.reshape(-1, value.shape[-1])
    padded = filled_up(lines, lax.axis_size(axes[0]) * lax.axis_size(axes[1]))
    whole = whole_of(sum_in_two_steps(padded, axes, 0), axes, 0)
    return lax.slice_in_dim(whole, 0, len(lines)).reshape(value.shape)


def total_of_2(value, axes):
    own = sum_in_two_steps(
        filled_up(value, lax.axis_size(axes[0]) * lax.axis_size(axes[1])), axes, 0
    )
    whole = whole_of(own, axes, 0)
    return whole[: len(value)].reshape(value.shape)


def in_one(arrays, axis):
    flat, at, done = (jnp.concatenate([a.reshape(-1) for a in arrays]), 0, [])
    running = total_of_2(flat, axis)
    for a in arrays:
        done.append(running[at : at + a.size].reshape(a.shape))
        at += a.size
    return tuple(done)


def staged_total(flat, axes):
    sizes = [lax.axis_size(a) for a in axes]
    devices = 1
    for n in sizes:
        devices *= n
    length = flat.shape[0]
    piece = -(-length // (devices * 128)) * 128
    part = jnp.pad(flat, (0, piece * devices - length))
    for axis, n in zip(axes, sizes):
        rows = part.reshape(n, -1, 128)
        part = jnp.sum(lax.all_to_all(rows, axis, 0, 0, tiled=True), axis=0).reshape(-1)
    for axis, n in zip(axes[::-1], sizes[::-1]):
        rows = jnp.broadcast_to(part.reshape(1, -1, 128), (n, part.shape[0] // 128, 128))
        part = lax.all_to_all(rows, axis, 0, 0, tiled=True).reshape(-1)
    return part[:length]


def split_parts(packed):
    flipped = jnp.swapaxes(packed, 1, 2)
    return jnp.stack([0.5 * (packed + flipped), 0.5 * (packed - flipped)])


def central(values, which_dim):
    padding = [(0, 0)] * values.ndim
    padding[which_dim] = (1, 1)
    padded = jnp.pad(values, padding)
    extent = values.shape[which_dim]
    return 0.5 * (
        lax.slice_in_dim(padded, 2, extent + 2, axis=which_dim)
        - lax.slice_in_dim(padded, 0, extent, axis=which_dim)
    )


def position_slopes(values):
    padded = padded_2(values, ((GX, 0),), 1)
    along_first = 0.5 * (padded[2:] - padded[:-2])
    return jnp.stack([along_first, central(values, 1), central(values, 2)])


def velocity_slopes(values):
    padded = extended(values, ((GX, 1), ("vert", 0)), 1)
    along_first = 0.5 * (padded[2:, 1:-1] - padded[:-2, 1:-1])
    along_second = 0.5 * (padded[1:-1, 2:] - padded[1:-1, :-2])
    return jnp.stack([along_first, along_second, central(values, 2)])


def coordinate(indices, cell_total):
    return (2.0 * indices.astype(jnp.float32) + 1.0 - cell_total) / cell_total


def velocity_grid(
    offset, slab_cells, first_count, second_offset, second_cells, second_count, third_count
):
    grid_shape = (slab_cells, second_cells, third_count)
    first_axis = coordinate(offset + jnp.arange(slab_cells, dtype=jnp.int32), first_count)
    second_axis = coordinate(
        second_offset + jnp.arange(second_cells, dtype=jnp.int32), second_count
    )
    third_axis = coordinate(jnp.arange(third_count, dtype=jnp.int32), third_count)
    return jnp.stack(
        [
            jnp.broadcast_to(first_axis[:, None, None], grid_shape),
            jnp.broadcast_to(second_axis[None, :, None], grid_shape),
            third_axis[None, None, :],
        ]
    )


def moments(factor, others, cells_count):
    return jnp.einsum("xyzr,dxyzs->drs", factor, others, precision=HIGHEST) / cells_count


def apply_pair(first_terms, first_mats, second_terms, second_mats):
    return -(
        jnp.einsum("dxyzs,drs->xyzr", first_terms, first_mats, precision=HIGHEST)
        + jnp.einsum("dxyzs,drs->xyzr", second_terms, second_mats, precision=HIGHEST)
    )


def newton_schulz(gram_matrix):
    frob_norm = jnp.sqrt(jnp.sum(gram_matrix * gram_matrix) + NORM_EPSILON)
    identity = jnp.eye(gram_matrix.shape[0], dtype=jnp.float32)
    root_part = gram_matrix / frob_norm
    inv_root = identity

    def sweep(_, carried):
        root_part, inv_root = carried
        middle = 1.5 * identity - 0.5 * jnp.dot(
            inv_root, root_part, precision=HIGHEST, preferred_element_type=jnp.float32
        )
        root_part = jnp.dot(
            root_part, middle, precision=HIGHEST, preferred_element_type=jnp.float32
        )
        inv_root = jnp.dot(middle, inv_root, precision=HIGHEST, preferred_element_type=jnp.float32)
        return root_part, inv_root

    root_part, inv_root = lax.fori_loop(0, NS_STEPS, sweep, (root_part, inv_root))
    scale_root = jnp.sqrt(frob_norm)
    return (inv_root / scale_root, root_part * scale_root)


def sandwich(left_mats, core_matrix, right_mats):
    return jnp.einsum("dij,jk,dlk->il", left_mats, core_matrix, right_mats, precision=HIGHEST)


def per_device(position_factor, coefficients, velocity_factor, gravity):
    slab_vel = velocity_factor.shape[0]
    column_vel = velocity_factor.shape[1]
    first_count = slab_vel * lax.axis_size("vert")
    second_count = column_vel * lax.axis_size(GX)
    pos_cells = (
        position_factor.shape[0]
        * lax.axis_size(GX)
        * position_factor.shape[1]
        * position_factor.shape[2]
    )
    vel_cells = first_count * second_count * velocity_factor.shape[2]
    offset = lax.axis_index("vert") * slab_vel
    second_offset = lax.axis_index(GX) * column_vel
    velocity = velocity_grid(
        offset,
        slab_vel,
        first_count,
        second_offset,
        column_vel,
        second_count,
        velocity_factor.shape[2],
    )
    vel_first = moments(velocity_factor, velocity[..., None] * velocity_factor[None], vel_cells)
    next_plane = from_behind(velocity_factor, "vert", -1)
    next_column = from_behind(velocity_factor, GX, -1)
    following = jnp.concatenate([velocity_factor[1:], next_plane], axis=0)
    beside = jnp.concatenate([velocity_factor[:, 1:], next_column], axis=1)
    pair_sums = jnp.stack(
        [
            jnp.einsum("xyzr,xyzs->rs", velocity_factor, following, precision=HIGHEST),
            jnp.einsum("xyzr,xyzs->rs", velocity_factor, beside, precision=HIGHEST),
            jnp.einsum(
                "xyzr,xyzs->rs",
                velocity_factor[:, :, :-1],
                velocity_factor[:, :, 1:],
                precision=HIGHEST,
            ),
        ]
    )
    vel_second = 0.5 * (pair_sums - jnp.swapaxes(pair_sums, 1, 2)) / vel_cells
    vel_packed = (vel_first + vel_second).reshape(-1)
    vel_mats = split_parts(
        staged_total(vel_packed, (("gx_1", "gx_2"), "vert", "gx_0")).reshape(vel_first.shape)
    )

    def position_rate(values):
        return apply_pair(
            position_slopes(values), vel_mats[0], gravity[..., None] * values[None], vel_mats[1]
        )

    initial = jnp.einsum("xyzs,sr->xyzr", position_factor, coefficients, precision=HIGHEST)
    section_one = initial + TIME_STEP * position_rate(initial)
    section_two = 0.75 * initial + 0.25 * (section_one + TIME_STEP * position_rate(section_one))
    final_section = 1.0 / 3.0 * initial + 2.0 / 3.0 * (
        section_two + TIME_STEP * position_rate(section_two)
    )
    gram_part = (
        jnp.einsum("xyzr,xyzs->rs", final_section, final_section, precision=HIGHEST) / pos_cells
    )
    raw_terms = jnp.stack(
        [
            moments(final_section, position_slopes(final_section), pos_cells),
            moments(final_section, gravity[..., None] * final_section[None], pos_cells),
        ]
    )
    local_packed = jnp.concatenate([gram_part[None], raw_terms[0] + raw_terms[1]])
    packed = staged_total(local_packed.reshape(-1), (("gx_1", "gx_2"), "gx_0")).reshape(
        local_packed.shape
    )
    gram_matrix = 0.5 * (packed[0] + packed[0].T)
    second_raw, first_raw = split_parts(packed[1:])
    summed_terms = jnp.stack([first_raw, second_raw])
    inv_root, root_part = newton_schulz(gram_matrix)
    new_position = jnp.einsum("xyzs,sr->xyzr", final_section, inv_root, precision=HIGHEST)
    pos_mats = jnp.einsum("ir,ndij,js->ndrs", inv_root, summed_terms, inv_root, precision=HIGHEST)
    coupled_core = root_part + TIME_STEP * (
        sandwich(pos_mats[0], root_part, vel_mats[0])
        + sandwich(pos_mats[1], root_part, vel_mats[1])
    )

    def velocity_rate(values):
        return apply_pair(
            velocity[..., None] * values[None], pos_mats[0], velocity_slopes(values), pos_mats[1]
        )

    vel_initial = jnp.einsum("abcs,rs->abcr", velocity_factor, coupled_core, precision=HIGHEST)
    vel_section = vel_initial + TIME_STEP * velocity_rate(vel_initial)
    new_velocity = 0.5 * vel_initial + 0.5 * (vel_section + TIME_STEP * velocity_rate(vel_section))
    return (new_position, new_velocity)


def solution(mesh):
    finer = Mesh(
        mesh.devices.reshape(8, 4, 2, mesh.shape["vert"]), ("gx_0", "gx_1", "gx_2", "vert")
    )
    in_specs = (P(GX, None, None, None), P(), P("vert", GX, None, None), P(None, GX, None, None))
    out_specs = (P(GX, None, None, None), P("vert", GX, None, None))
    return jax.shard_map(
        per_device, mesh=finer, in_specs=in_specs, out_specs=out_specs, check_vma=False
    )
```

```python
import jax
import jax.numpy as jnp
from jax import lax
from jax.sharding import Mesh
from jax.sharding import PartitionSpec as P

NS_STEPS = 8
GX = ("gx_0", "gx_1", "gx_2")


HIGHEST = lax.Precision.HIGHEST
TIME_STEP = 0.25
NORM_EPSILON = 1e-06


def padded_2(block, sides, width):
    for axis, dim in sides:
        count = lax.axis_size(axis)
        forward = [(i, i + 1) for i in range(count - 1)]
        backward = [(target, source) for source, target in forward]
        low = lax.ppermute(
            lax.slice_in_dim(block, block.shape[dim] - width, None, axis=dim), axis, forward
        )
        high = lax.ppermute(lax.slice_in_dim(block, 0, width, axis=dim), axis, backward)
        block = jnp.concatenate([low, block, high], axis=dim)
    return block


def extended(value, sides, width):
    edges = {}
    for axis, dim in sides:
        devices, length = (lax.axis_size(axis), value.shape[dim])
        up = [(i, (i + 1) % devices) for i in range(devices - 1)]
        last = lax.slice_in_dim(value, length - width, length, axis=dim)
        first = lax.slice_in_dim(value, 0, width, axis=dim)
        edges[dim] = (
            lax.ppermute(last, axis, up),
            lax.ppermute(first, axis, [(b, a) for a, b in up]),
        )
    done = []
    for _, dim in sides:
        low, high = edges[dim]
        around = [(width, width) if d in done else (0, 0) for d in range(value.ndim)]
        value = jnp.concatenate([jnp.pad(low, around), value, jnp.pad(high, around)], axis=dim)
        done.append(dim)
    return value


def from_behind(block, axis, distance):
    devices = range(lax.axis_size(axis))
    route = [(i - distance, i) for i in devices if i - distance in devices]
    return lax.ppermute(block, axis, route)


def filled_up(lines, devices):
    spare = -len(lines) % devices
    return jnp.pad(lines, [(0, spare)] + [(0, 0)] * (lines.ndim - 1))


def from_everyone(value, axis):
    devices = lax.axis_size(axis)
    return lax.all_to_all(
        jnp.broadcast_to(value[None], (devices, *value.shape)), axis, 0, 0, tiled=True
    )


def laid_out(pieces, dim):
    dims = list(pieces.shape[1:])
    dims[dim] *= pieces.shape[0]
    return jnp.moveaxis(pieces, 0, dim).reshape(dims)


def whole_of(value, axes, dim):
    far, near = axes
    pieces = from_everyone(from_everyone(value, far), near)
    return laid_out(pieces.swapaxes(0, 1).reshape(-1, *value.shape), dim)


def split_up(value, dim, devices):
    dims = value.shape
    pieces = value.reshape(*dims[:dim], devices, dims[dim] // devices, *dims[dim + 1 :])
    return jnp.moveaxis(pieces, dim, 0)


def sum_at_owner(value, axis, dim):
    devices = lax.axis_size(axis)
    pieces = lax.all_to_all(split_up(value, dim, devices), axis, 0, 0, tiled=True)
    return jnp.sum(pieces, axis=0)


def sum_in_two_steps(value, axes, dim):
    far, near = axes
    own = sum_at_owner(split_up(value, dim, lax.axis_size(far)), near, dim + 1)
    return jnp.sum(lax.all_to_all(own, far, 0, 0, tiled=True), axis=0)


def total_of(value, axes):
    lines = value.reshape(-1, value.shape[-1])
    padded = filled_up(lines, lax.axis_size(axes[0]) * lax.axis_size(axes[1]))
    whole = whole_of(sum_in_two_steps(padded, axes, 0), axes, 0)
    return lax.slice_in_dim(whole, 0, len(lines)).reshape(value.shape)


def total_of_2(value, axes):
    own = sum_in_two_steps(
        filled_up(value, lax.axis_size(axes[0]) * lax.axis_size(axes[1])), axes, 0
    )
    whole = whole_of(own, axes, 0)
    return whole[: len(value)].reshape(value.shape)


def in_one(arrays, axis):
    flat, at, done = (jnp.concatenate([a.reshape(-1) for a in arrays]), 0, [])
    running = total_of_2(flat, axis)
    for a in arrays:
        done.append(running[at : at + a.size].reshape(a.shape))
        at += a.size
    return tuple(done)


def staged_total(flat, axes):
    sizes = [lax.axis_size(a) for a in axes]
    devices = 1
    for n in sizes:
        devices *= n
    length = flat.shape[0]
    piece = -(-length // (devices * 128)) * 128
    part = jnp.pad(flat, (0, piece * devices - length))
    for axis, n in zip(axes, sizes):
        rows = part.reshape(n, -1, 128)
        part = jnp.sum(lax.all_to_all(rows, axis, 0, 0, tiled=True), axis=0).reshape(-1)
    for axis, n in zip(axes[::-1], sizes[::-1]):
        rows = jnp.broadcast_to(part.reshape(1, -1, 128), (n, part.shape[0] // 128, 128))
        part = lax.all_to_all(rows, axis, 0, 0, tiled=True).reshape(-1)
    return part[:length]


def split_parts(packed):
    flipped = jnp.swapaxes(packed, 1, 2)
    return jnp.stack([0.5 * (packed + flipped), 0.5 * (packed - flipped)])


def central(values, which_dim):
    padding = [(0, 0)] * values.ndim
    padding[which_dim] = (1, 1)
    padded = jnp.pad(values, padding)
    extent = values.shape[which_dim]
    return 0.5 * (
        lax.slice_in_dim(padded, 2, extent + 2, axis=which_dim)
        - lax.slice_in_dim(padded, 0, extent, axis=which_dim)
    )


def final_first_moments(values, cells):
    ahead = from_behind(values, GX, -1)
    following = jnp.concatenate([values[1:], ahead], axis=0)
    pairs = jnp.einsum("xyzr,xyzs->rs", values, following, precision=HIGHEST)
    across = 0.5 * (pairs - pairs.T)
    within = jnp.einsum(
        "xyzr,dxyzs->drs",
        values,
        jnp.stack([central(values, 1), central(values, 2)]),
        precision=HIGHEST,
    )
    return jnp.concatenate([across[None], within]) / cells


def position_slopes(values):
    padded = padded_2(values, ((GX, 0),), 1)
    along_first = 0.5 * (padded[2:] - padded[:-2])
    return jnp.stack([along_first, central(values, 1), central(values, 2)])


def velocity_slopes(values):
    padded = extended(values, ((GX, 1), ("vert", 0)), 1)
    along_first = 0.5 * (padded[2:, 1:-1] - padded[:-2, 1:-1])
    along_second = 0.5 * (padded[1:-1, 2:] - padded[1:-1, :-2])
    return jnp.stack([along_first, along_second, central(values, 2)])


def coordinate(indices, cell_total):
    return (2.0 * indices.astype(jnp.float32) + 1.0 - cell_total) / cell_total


def velocity_grid(
    offset, slab_cells, first_count, second_offset, second_cells, second_count, third_count
):
    grid_shape = (slab_cells, second_cells, third_count)
    first_axis = coordinate(offset + jnp.arange(slab_cells, dtype=jnp.int32), first_count)
    second_axis = coordinate(
        second_offset + jnp.arange(second_cells, dtype=jnp.int32), second_count
    )
    third_axis = coordinate(jnp.arange(third_count, dtype=jnp.int32), third_count)
    return jnp.stack(
        [
            jnp.broadcast_to(first_axis[:, None, None], grid_shape),
            jnp.broadcast_to(second_axis[None, :, None], grid_shape),
            third_axis[None, None, :],
        ]
    )


def moments(factor, others, cells_count):
    return jnp.einsum("xyzr,dxyzs->drs", factor, others, precision=HIGHEST) / cells_count


def apply_pair(first_terms, first_mats, second_terms, second_mats):
    return -(
        jnp.einsum("dxyzs,drs->xyzr", first_terms, first_mats, precision=HIGHEST)
        + jnp.einsum("dxyzs,drs->xyzr", second_terms, second_mats, precision=HIGHEST)
    )


def newton_schulz(gram_matrix):
    frob_norm = jnp.sqrt(jnp.sum(gram_matrix * gram_matrix) + NORM_EPSILON)
    identity = jnp.eye(gram_matrix.shape[0], dtype=jnp.float32)
    root_part = gram_matrix / frob_norm
    inv_root = identity
    for sweep_index in range(NS_STEPS):
        middle = 1.5 * identity - 0.5 * jnp.dot(
            inv_root, root_part, precision=HIGHEST, preferred_element_type=jnp.float32
        )
        root_part = jnp.dot(
            root_part, middle, precision=HIGHEST, preferred_element_type=jnp.float32
        )
        inv_root = jnp.dot(middle, inv_root, precision=HIGHEST, preferred_element_type=jnp.float32)
    scale_root = jnp.sqrt(frob_norm)
    return (inv_root / scale_root, root_part * scale_root)


def sandwich(left_mats, core_matrix, right_mats):
    return jnp.einsum("dij,jk,dlk->il", left_mats, core_matrix, right_mats, precision=HIGHEST)


def per_device(position_factor, coefficients, velocity_factor, gravity):
    slab_vel = velocity_factor.shape[0]
    column_vel = velocity_factor.shape[1]
    first_count = slab_vel * lax.axis_size("vert")
    second_count = column_vel * lax.axis_size(GX)
    pos_cells = (
        position_factor.shape[0]
        * lax.axis_size(GX)
        * position_factor.shape[1]
        * position_factor.shape[2]
    )
    vel_cells = first_count * second_count * velocity_factor.shape[2]
    offset = lax.axis_index("vert") * slab_vel
    second_offset = lax.axis_index(GX) * column_vel
    velocity = velocity_grid(
        offset,
        slab_vel,
        first_count,
        second_offset,
        column_vel,
        second_count,
        velocity_factor.shape[2],
    )
    vel_first = moments(velocity_factor, velocity[..., None] * velocity_factor[None], vel_cells)
    next_plane = from_behind(velocity_factor, "vert", -1)
    next_column = from_behind(velocity_factor, GX, -1)
    following = jnp.concatenate([velocity_factor[1:], next_plane], axis=0)
    beside = jnp.concatenate([velocity_factor[:, 1:], next_column], axis=1)
    pair_sums = jnp.stack(
        [
            jnp.einsum("xyzr,xyzs->rs", velocity_factor, following, precision=HIGHEST),
            jnp.einsum("xyzr,xyzs->rs", velocity_factor, beside, precision=HIGHEST),
            jnp.einsum(
                "xyzr,xyzs->rs",
                velocity_factor[:, :, :-1],
                velocity_factor[:, :, 1:],
                precision=HIGHEST,
            ),
        ]
    )
    vel_second = 0.5 * (pair_sums - jnp.swapaxes(pair_sums, 1, 2)) / vel_cells
    vel_packed = (vel_first + vel_second).reshape(-1)
    vel_mats = split_parts(
        staged_total(vel_packed, (("gx_1", "gx_2"), "vert", "gx_0")).reshape(vel_first.shape)
    )

    def position_rate(values):
        return apply_pair(
            position_slopes(values), vel_mats[0], gravity[..., None] * values[None], vel_mats[1]
        )

    initial = jnp.einsum("xyzs,sr->xyzr", position_factor, coefficients, precision=HIGHEST)
    section_one = initial + TIME_STEP * position_rate(initial)
    section_two = 0.75 * initial + 0.25 * (section_one + TIME_STEP * position_rate(section_one))
    final_section = 1.0 / 3.0 * initial + 2.0 / 3.0 * (
        section_two + TIME_STEP * position_rate(section_two)
    )
    gram_part = (
        jnp.einsum("xyzr,xyzs->rs", final_section, final_section, precision=HIGHEST) / pos_cells
    )
    raw_terms = jnp.stack(
        [
            final_first_moments(final_section, pos_cells),
            moments(final_section, gravity[..., None] * final_section[None], pos_cells),
        ]
    )
    local_packed = jnp.concatenate([gram_part[None], raw_terms[0] + raw_terms[1]])
    packed = staged_total(local_packed.reshape(-1), ("gx_2", ("gx_0", "gx_1"))).reshape(
        local_packed.shape
    )
    gram_matrix = 0.5 * (packed[0] + packed[0].T)
    second_raw, first_raw = split_parts(packed[1:])
    summed_terms = jnp.stack([first_raw, second_raw])
    inv_root, root_part = newton_schulz(gram_matrix)
    new_position = jnp.einsum("xyzs,sr->xyzr", final_section, inv_root, precision=HIGHEST)
    pos_mats = jnp.einsum("ir,ndij,js->ndrs", inv_root, summed_terms, inv_root, precision=HIGHEST)
    coupled_core = root_part + TIME_STEP * (
        sandwich(pos_mats[0], root_part, vel_mats[0])
        + sandwich(pos_mats[1], root_part, vel_mats[1])
    )

    def velocity_rate(values):
        return apply_pair(
            velocity[..., None] * values[None], pos_mats[0], velocity_slopes(values), pos_mats[1]
        )

    vel_initial = jnp.einsum("abcs,rs->abcr", velocity_factor, coupled_core, precision=HIGHEST)
    vel_section = vel_initial + TIME_STEP * velocity_rate(vel_initial)
    new_velocity = 0.5 * vel_initial + 0.5 * (vel_section + TIME_STEP * velocity_rate(vel_section))
    return (new_position, new_velocity)


def solution(mesh):
    finer = Mesh(
        mesh.devices.reshape(8, 4, 2, mesh.shape["vert"]), ("gx_0", "gx_1", "gx_2", "vert")
    )
    in_specs = (P(GX, None, None, None), P(), P("vert", GX, None, None), P(None, GX, None, None))
    out_specs = (P(GX, None, None, None), P("vert", GX, None, None))
    return jax.shard_map(
        per_device, mesh=finer, in_specs=in_specs, out_specs=out_specs, check_vma=False
    )
```

```python
import jax
import jax.numpy as jnp
from jax import lax
from jax.sharding import Mesh
from jax.sharding import PartitionSpec as P

NS_STEPS = 8
GX = ("gx_0", "gx_1", "gx_2")


HIGHEST = lax.Precision.HIGHEST
TIME_STEP = 0.25
NORM_EPSILON = 1e-06


def padded_2(block, sides, width):
    for axis, dim in sides:
        count = lax.axis_size(axis)
        forward = [(i, i + 1) for i in range(count - 1)]
        backward = [(target, source) for source, target in forward]
        low = lax.ppermute(
            lax.slice_in_dim(block, block.shape[dim] - width, None, axis=dim), axis, forward
        )
        high = lax.ppermute(lax.slice_in_dim(block, 0, width, axis=dim), axis, backward)
        block = jnp.concatenate([low, block, high], axis=dim)
    return block


def extended(value, sides, width):
    edges = {}
    for axis, dim in sides:
        devices, length = (lax.axis_size(axis), value.shape[dim])
        up = [(i, (i + 1) % devices) for i in range(devices - 1)]
        last = lax.slice_in_dim(value, length - width, length, axis=dim)
        first = lax.slice_in_dim(value, 0, width, axis=dim)
        edges[dim] = (
            lax.ppermute(last, axis, up),
            lax.ppermute(first, axis, [(b, a) for a, b in up]),
        )
    done = []
    for _, dim in sides:
        low, high = edges[dim]
        around = [(width, width) if d in done else (0, 0) for d in range(value.ndim)]
        value = jnp.concatenate([jnp.pad(low, around), value, jnp.pad(high, around)], axis=dim)
        done.append(dim)
    return value


def from_behind(block, axis, distance):
    devices = range(lax.axis_size(axis))
    route = [(i - distance, i) for i in devices if i - distance in devices]
    return lax.ppermute(block, axis, route)


def filled_up(lines, devices):
    spare = -len(lines) % devices
    return jnp.pad(lines, [(0, spare)] + [(0, 0)] * (lines.ndim - 1))


def from_everyone(value, axis):
    devices = lax.axis_size(axis)
    return lax.all_to_all(
        jnp.broadcast_to(value[None], (devices, *value.shape)), axis, 0, 0, tiled=True
    )


def laid_out(pieces, dim):
    dims = list(pieces.shape[1:])
    dims[dim] *= pieces.shape[0]
    return jnp.moveaxis(pieces, 0, dim).reshape(dims)


def whole_of(value, axes, dim):
    far, near = axes
    pieces = from_everyone(from_everyone(value, far), near)
    return laid_out(pieces.swapaxes(0, 1).reshape(-1, *value.shape), dim)


def split_up(value, dim, devices):
    dims = value.shape
    pieces = value.reshape(*dims[:dim], devices, dims[dim] // devices, *dims[dim + 1 :])
    return jnp.moveaxis(pieces, dim, 0)


def sum_at_owner(value, axis, dim):
    devices = lax.axis_size(axis)
    pieces = lax.all_to_all(split_up(value, dim, devices), axis, 0, 0, tiled=True)
    return jnp.sum(pieces, axis=0)


def sum_in_two_steps(value, axes, dim):
    far, near = axes
    own = sum_at_owner(split_up(value, dim, lax.axis_size(far)), near, dim + 1)
    return jnp.sum(lax.all_to_all(own, far, 0, 0, tiled=True), axis=0)


def total_of(value, axes):
    lines = value.reshape(-1, value.shape[-1])
    padded = filled_up(lines, lax.axis_size(axes[0]) * lax.axis_size(axes[1]))
    whole = whole_of(sum_in_two_steps(padded, axes, 0), axes, 0)
    return lax.slice_in_dim(whole, 0, len(lines)).reshape(value.shape)


def total_of_2(value, axes):
    own = sum_in_two_steps(
        filled_up(value, lax.axis_size(axes[0]) * lax.axis_size(axes[1])), axes, 0
    )
    whole = whole_of(own, axes, 0)
    return whole[: len(value)].reshape(value.shape)


def in_one(arrays, axis):
    flat, at, done = (jnp.concatenate([a.reshape(-1) for a in arrays]), 0, [])
    running = total_of_2(flat, axis)
    for a in arrays:
        done.append(running[at : at + a.size].reshape(a.shape))
        at += a.size
    return tuple(done)


def staged_total(flat, axes):
    sizes = [lax.axis_size(a) for a in axes]
    devices = 1
    for n in sizes:
        devices *= n
    length = flat.shape[0]
    piece = -(-length // (devices * 128)) * 128
    part = jnp.pad(flat, (0, piece * devices - length))
    for axis, n in zip(axes, sizes):
        rows = part.reshape(n, -1, 128)
        part = jnp.sum(lax.all_to_all(rows, axis, 0, 0, tiled=True), axis=0).reshape(-1)
    for axis, n in zip(axes[::-1], sizes[::-1]):
        rows = jnp.broadcast_to(part.reshape(1, -1, 128), (n, part.shape[0] // 128, 128))
        part = lax.all_to_all(rows, axis, 0, 0, tiled=True).reshape(-1)
    return part[:length]


def split_parts(packed):
    flipped = jnp.swapaxes(packed, 1, 2)
    return jnp.stack([0.5 * (packed + flipped), 0.5 * (packed - flipped)])


def central(values, which_dim):
    padding = [(0, 0)] * values.ndim
    padding[which_dim] = (1, 1)
    padded = jnp.pad(values, padding)
    extent = values.shape[which_dim]
    return 0.5 * (
        lax.slice_in_dim(padded, 2, extent + 2, axis=which_dim)
        - lax.slice_in_dim(padded, 0, extent, axis=which_dim)
    )


def final_first_moments(values, cells):
    ahead = from_behind(values, GX, -1)
    following = jnp.concatenate([values[1:], ahead], axis=0)
    pairs = jnp.einsum("xyzr,xyzs->rs", values, following, precision=HIGHEST)
    across = 0.5 * (pairs - pairs.T)
    within = jnp.einsum(
        "xyzr,dxyzs->drs",
        values,
        jnp.stack([central(values, 1), central(values, 2)]),
        precision=HIGHEST,
    )
    return jnp.concatenate([across[None], within]) / cells


def position_slopes(values):
    padded = padded_2(values, ((GX, 0),), 1)
    along_first = 0.5 * (padded[2:] - padded[:-2])
    return jnp.stack([along_first, central(values, 1), central(values, 2)])


def velocity_slopes(values):
    padded = extended(values, ((GX, 1), ("vert", 0)), 1)
    along_first = 0.5 * (padded[2:, 1:-1] - padded[:-2, 1:-1])
    along_second = 0.5 * (padded[1:-1, 2:] - padded[1:-1, :-2])
    return jnp.stack([along_first, along_second, central(values, 2)])


def coordinate(indices, cell_total):
    return (2.0 * indices.astype(jnp.float32) + 1.0 - cell_total) / cell_total


def velocity_grid(
    offset, slab_cells, first_count, second_offset, second_cells, second_count, third_count
):
    grid_shape = (slab_cells, second_cells, third_count)
    first_axis = coordinate(offset + jnp.arange(slab_cells, dtype=jnp.int32), first_count)
    second_axis = coordinate(
        second_offset + jnp.arange(second_cells, dtype=jnp.int32), second_count
    )
    third_axis = coordinate(jnp.arange(third_count, dtype=jnp.int32), third_count)
    return jnp.stack(
        [
            jnp.broadcast_to(first_axis[:, None, None], grid_shape),
            jnp.broadcast_to(second_axis[None, :, None], grid_shape),
            third_axis[None, None, :],
        ]
    )


def moments(factor, others, cells_count):
    return jnp.einsum("xyzr,dxyzs->drs", factor, others, precision=HIGHEST) / cells_count


def apply_pair(first_terms, first_mats, second_terms, second_mats):
    return -(
        jnp.einsum("dxyzs,drs->xyzr", first_terms, first_mats, precision=HIGHEST)
        + jnp.einsum("dxyzs,drs->xyzr", second_terms, second_mats, precision=HIGHEST)
    )


def newton_schulz(gram_matrix):
    frob_norm = jnp.sqrt(jnp.sum(gram_matrix * gram_matrix) + NORM_EPSILON)
    identity = jnp.eye(gram_matrix.shape[0], dtype=jnp.float32)
    root_part = gram_matrix / frob_norm
    inv_root = identity
    for sweep_index in range(NS_STEPS):
        middle = 1.5 * identity - 0.5 * jnp.dot(
            inv_root, root_part, precision=HIGHEST, preferred_element_type=jnp.float32
        )
        root_part = jnp.dot(
            root_part, middle, precision=HIGHEST, preferred_element_type=jnp.float32
        )
        inv_root = jnp.dot(middle, inv_root, precision=HIGHEST, preferred_element_type=jnp.float32)
    scale_root = jnp.sqrt(frob_norm)
    return (inv_root / scale_root, root_part * scale_root)


def sandwich(left_mats, core_matrix, right_mats):
    return jnp.einsum("dij,jk,dlk->il", left_mats, core_matrix, right_mats, precision=HIGHEST)


def per_device(position_factor, coefficients, velocity_factor, gravity):
    slab_vel = velocity_factor.shape[0]
    column_vel = velocity_factor.shape[1]
    first_count = slab_vel * lax.axis_size("vert")
    second_count = column_vel * lax.axis_size(GX)
    pos_cells = (
        position_factor.shape[0]
        * lax.axis_size(GX)
        * position_factor.shape[1]
        * position_factor.shape[2]
    )
    vel_cells = first_count * second_count * velocity_factor.shape[2]
    offset = lax.axis_index("vert") * slab_vel
    second_offset = lax.axis_index(GX) * column_vel
    velocity = velocity_grid(
        offset,
        slab_vel,
        first_count,
        second_offset,
        column_vel,
        second_count,
        velocity_factor.shape[2],
    )
    vel_first = moments(velocity_factor, velocity[..., None] * velocity_factor[None], vel_cells)
    next_plane = from_behind(velocity_factor, "vert", -1)
    next_column = from_behind(velocity_factor, GX, -1)
    following = jnp.concatenate([velocity_factor[1:], next_plane], axis=0)
    beside = jnp.concatenate([velocity_factor[:, 1:], next_column], axis=1)
    pair_sums = jnp.stack(
        [
            jnp.einsum("xyzr,xyzs->rs", velocity_factor, following, precision=HIGHEST),
            jnp.einsum("xyzr,xyzs->rs", velocity_factor, beside, precision=HIGHEST),
            jnp.einsum(
                "xyzr,xyzs->rs",
                velocity_factor[:, :, :-1],
                velocity_factor[:, :, 1:],
                precision=HIGHEST,
            ),
        ]
    )
    vel_second = 0.5 * (pair_sums - jnp.swapaxes(pair_sums, 1, 2)) / vel_cells
    vel_packed = (vel_first + vel_second).reshape(-1)
    vel_mats = split_parts(
        staged_total(vel_packed, (("gx_1", "gx_2"), ("gx_0", "vert"))).reshape(vel_first.shape)
    )

    def position_rate(values):
        return apply_pair(
            position_slopes(values), vel_mats[0], gravity[..., None] * values[None], vel_mats[1]
        )

    initial = jnp.einsum("xyzs,sr->xyzr", position_factor, coefficients, precision=HIGHEST)
    section_one = initial + TIME_STEP * position_rate(initial)
    section_two = 0.75 * initial + 0.25 * (section_one + TIME_STEP * position_rate(section_one))
    final_section = 1.0 / 3.0 * initial + 2.0 / 3.0 * (
        section_two + TIME_STEP * position_rate(section_two)
    )
    gram_part = (
        jnp.einsum("xyzr,xyzs->rs", final_section, final_section, precision=HIGHEST) / pos_cells
    )
    raw_terms = jnp.stack(
        [
            final_first_moments(final_section, pos_cells),
            moments(final_section, gravity[..., None] * final_section[None], pos_cells),
        ]
    )
    local_packed = jnp.concatenate([gram_part[None], raw_terms[0] + raw_terms[1]])
    packed = staged_total(local_packed.reshape(-1), ("gx_2", ("gx_0", "gx_1"))).reshape(
        local_packed.shape
    )
    gram_matrix = 0.5 * (packed[0] + packed[0].T)
    second_raw, first_raw = split_parts(packed[1:])
    summed_terms = jnp.stack([first_raw, second_raw])
    inv_root, root_part = newton_schulz(gram_matrix)
    new_position = jnp.einsum("xyzs,sr->xyzr", final_section, inv_root, precision=HIGHEST)
    pos_mats = jnp.einsum("ir,ndij,js->ndrs", inv_root, summed_terms, inv_root, precision=HIGHEST)
    coupled_core = root_part + TIME_STEP * (
        sandwich(pos_mats[0], root_part, vel_mats[0])
        + sandwich(pos_mats[1], root_part, vel_mats[1])
    )

    def velocity_rate(values):
        return apply_pair(
            velocity[..., None] * values[None], pos_mats[0], velocity_slopes(values), pos_mats[1]
        )

    vel_initial = jnp.einsum("abcs,rs->abcr", velocity_factor, coupled_core, precision=HIGHEST)
    vel_section = vel_initial + TIME_STEP * velocity_rate(vel_initial)
    new_velocity = 0.5 * vel_initial + 0.5 * (vel_section + TIME_STEP * velocity_rate(vel_section))
    return (new_position, new_velocity)


def solution(mesh):
    finer = Mesh(
        mesh.devices.reshape(8, 4, 2, mesh.shape["vert"]), ("gx_0", "gx_1", "gx_2", "vert")
    )
    in_specs = (P(GX, None, None, None), P(), P("vert", GX, None, None), P(None, GX, None, None))
    out_specs = (P(GX, None, None, None), P("vert", GX, None, None))
    return jax.shard_map(
        per_device, mesh=finer, in_specs=in_specs, out_specs=out_specs, check_vma=False
    )
```

```python
import jax
import jax.numpy as jnp
from jax import lax
from jax.sharding import Mesh
from jax.sharding import PartitionSpec as P

NS_STEPS = 8
GX = ("gx_0", "gx_1", "gx_2")


HIGHEST = lax.Precision.HIGHEST
TIME_STEP = 0.25
NORM_EPSILON = 1e-06


def padded_2(block, sides, width):
    for axis, dim in sides:
        count = lax.axis_size(axis)
        forward = [(i, i + 1) for i in range(count - 1)]
        backward = [(target, source) for source, target in forward]
        low = lax.ppermute(
            lax.slice_in_dim(block, block.shape[dim] - width, None, axis=dim), axis, forward
        )
        high = lax.ppermute(lax.slice_in_dim(block, 0, width, axis=dim), axis, backward)
        block = jnp.concatenate([low, block, high], axis=dim)
    return block


def extended(value, sides, width):
    edges = {}
    for axis, dim in sides:
        devices, length = (lax.axis_size(axis), value.shape[dim])
        up = [(i, (i + 1) % devices) for i in range(devices - 1)]
        last = lax.slice_in_dim(value, length - width, length, axis=dim)
        first = lax.slice_in_dim(value, 0, width, axis=dim)
        edges[dim] = (
            lax.ppermute(last, axis, up),
            lax.ppermute(first, axis, [(b, a) for a, b in up]),
        )
    done = []
    for _, dim in sides:
        low, high = edges[dim]
        around = [(width, width) if d in done else (0, 0) for d in range(value.ndim)]
        value = jnp.concatenate([jnp.pad(low, around), value, jnp.pad(high, around)], axis=dim)
        done.append(dim)
    return value


def from_behind(block, axis, distance):
    devices = range(lax.axis_size(axis))
    route = [(i - distance, i) for i in devices if i - distance in devices]
    return lax.ppermute(block, axis, route)


def filled_up(lines, devices):
    spare = -len(lines) % devices
    return jnp.pad(lines, [(0, spare)] + [(0, 0)] * (lines.ndim - 1))


def from_everyone(value, axis):
    devices = lax.axis_size(axis)
    return lax.all_to_all(
        jnp.broadcast_to(value[None], (devices, *value.shape)), axis, 0, 0, tiled=True
    )


def laid_out(pieces, dim):
    dims = list(pieces.shape[1:])
    dims[dim] *= pieces.shape[0]
    return jnp.moveaxis(pieces, 0, dim).reshape(dims)


def whole_of(value, axes, dim):
    far, near = axes
    pieces = from_everyone(from_everyone(value, far), near)
    return laid_out(pieces.swapaxes(0, 1).reshape(-1, *value.shape), dim)


def split_up(value, dim, devices):
    dims = value.shape
    pieces = value.reshape(*dims[:dim], devices, dims[dim] // devices, *dims[dim + 1 :])
    return jnp.moveaxis(pieces, dim, 0)


def sum_at_owner(value, axis, dim):
    devices = lax.axis_size(axis)
    pieces = lax.all_to_all(split_up(value, dim, devices), axis, 0, 0, tiled=True)
    return jnp.sum(pieces, axis=0)


def sum_in_two_steps(value, axes, dim):
    far, near = axes
    own = sum_at_owner(split_up(value, dim, lax.axis_size(far)), near, dim + 1)
    return jnp.sum(lax.all_to_all(own, far, 0, 0, tiled=True), axis=0)


def total_of(value, axes):
    lines = value.reshape(-1, value.shape[-1])
    padded = filled_up(lines, lax.axis_size(axes[0]) * lax.axis_size(axes[1]))
    whole = whole_of(sum_in_two_steps(padded, axes, 0), axes, 0)
    return lax.slice_in_dim(whole, 0, len(lines)).reshape(value.shape)


def total_of_2(value, axes):
    own = sum_in_two_steps(
        filled_up(value, lax.axis_size(axes[0]) * lax.axis_size(axes[1])), axes, 0
    )
    whole = whole_of(own, axes, 0)
    return whole[: len(value)].reshape(value.shape)


def in_one(arrays, axis):
    flat, at, done = (jnp.concatenate([a.reshape(-1) for a in arrays]), 0, [])
    running = total_of_2(flat, axis)
    for a in arrays:
        done.append(running[at : at + a.size].reshape(a.shape))
        at += a.size
    return tuple(done)


def staged_total(flat, axes):
    sizes = [lax.axis_size(a) for a in axes]
    devices = 1
    for n in sizes:
        devices *= n
    length = flat.shape[0]
    piece = -(-length // (devices * 128)) * 128
    part = jnp.pad(flat, (0, piece * devices - length))
    for axis, n in zip(axes, sizes):
        rows = part.reshape(n, -1, 128)
        part = jnp.sum(lax.all_to_all(rows, axis, 0, 0, tiled=True), axis=0).reshape(-1)
    for axis, n in zip(axes[::-1], sizes[::-1]):
        rows = jnp.broadcast_to(part.reshape(1, -1, 128), (n, part.shape[0] // 128, 128))
        part = lax.all_to_all(rows, axis, 0, 0, tiled=True).reshape(-1)
    return part[:length]


def split_parts(packed):
    flipped = jnp.swapaxes(packed, 1, 2)
    return jnp.stack([0.5 * (packed + flipped), 0.5 * (packed - flipped)])


def central(values, which_dim):
    padding = [(0, 0)] * values.ndim
    padding[which_dim] = (1, 1)
    padded = jnp.pad(values, padding)
    extent = values.shape[which_dim]
    return 0.5 * (
        lax.slice_in_dim(padded, 2, extent + 2, axis=which_dim)
        - lax.slice_in_dim(padded, 0, extent, axis=which_dim)
    )


def final_first_moments(values, cells):
    ahead = from_behind(values, GX, -1)
    following = jnp.concatenate([values[1:], ahead], axis=0)
    pairs = jnp.einsum("xyzr,xyzs->rs", values, following, precision=HIGHEST)
    across = 0.5 * (pairs - pairs.T)
    within = jnp.einsum(
        "xyzr,dxyzs->drs",
        values,
        jnp.stack([central(values, 1), central(values, 2)]),
        precision=HIGHEST,
    )
    return jnp.concatenate([across[None], within]) / cells


def position_slopes(values):
    padded = padded_2(values, ((GX, 0),), 1)
    along_first = 0.5 * (padded[2:] - padded[:-2])
    return jnp.stack([along_first, central(values, 1), central(values, 2)])


def velocity_slopes(values):
    padded = extended(values, ((GX, 1), ("vert", 0)), 1)
    along_first = 0.5 * (padded[2:, 1:-1] - padded[:-2, 1:-1])
    along_second = 0.5 * (padded[1:-1, 2:] - padded[1:-1, :-2])
    return jnp.stack([along_first, along_second, central(values, 2)])


def coordinate(indices, cell_total):
    return (2.0 * indices.astype(jnp.float32) + 1.0 - cell_total) / cell_total


def velocity_grid(
    offset, slab_cells, first_count, second_offset, second_cells, second_count, third_count
):
    grid_shape = (slab_cells, second_cells, third_count)
    first_axis = coordinate(offset + jnp.arange(slab_cells, dtype=jnp.int32), first_count)
    second_axis = coordinate(
        second_offset + jnp.arange(second_cells, dtype=jnp.int32), second_count
    )
    third_axis = coordinate(jnp.arange(third_count, dtype=jnp.int32), third_count)
    return jnp.stack(
        [
            jnp.broadcast_to(first_axis[:, None, None], grid_shape),
            jnp.broadcast_to(second_axis[None, :, None], grid_shape),
            third_axis[None, None, :],
        ]
    )


def moments(factor, others, cells_count):
    return jnp.einsum("xyzr,dxyzs->drs", factor, others, precision=HIGHEST) / cells_count


def apply_pair(first_terms, first_mats, second_terms, second_mats):
    return -(
        jnp.einsum("dxyzs,drs->xyzr", first_terms, first_mats, precision=HIGHEST)
        + jnp.einsum("dxyzs,drs->xyzr", second_terms, second_mats, precision=HIGHEST)
    )


def newton_schulz(gram_matrix):
    frob_norm = jnp.sqrt(jnp.sum(gram_matrix * gram_matrix) + NORM_EPSILON)
    identity = jnp.eye(gram_matrix.shape[0], dtype=jnp.float32)
    root_part = gram_matrix / frob_norm
    inv_root = identity
    for sweep_index in range(NS_STEPS):
        middle = 1.5 * identity - 0.5 * jnp.dot(
            inv_root, root_part, precision=HIGHEST, preferred_element_type=jnp.float32
        )
        root_part = jnp.dot(
            root_part, middle, precision=HIGHEST, preferred_element_type=jnp.float32
        )
        inv_root = jnp.dot(middle, inv_root, precision=HIGHEST, preferred_element_type=jnp.float32)
    scale_root = jnp.sqrt(frob_norm)
    return (inv_root / scale_root, root_part * scale_root)


def sandwich(left_mats, core_matrix, right_mats):
    return jnp.einsum("dij,jk,dlk->il", left_mats, core_matrix, right_mats, precision=HIGHEST)


def per_device(position_factor, coefficients, velocity_factor, gravity):
    slab_vel = velocity_factor.shape[0]
    column_vel = velocity_factor.shape[1]
    first_count = slab_vel * lax.axis_size("vert")
    second_count = column_vel * lax.axis_size(GX)
    pos_cells = (
        position_factor.shape[0]
        * lax.axis_size(GX)
        * position_factor.shape[1]
        * position_factor.shape[2]
    )
    vel_cells = first_count * second_count * velocity_factor.shape[2]
    offset = lax.axis_index("vert") * slab_vel
    second_offset = lax.axis_index(GX) * column_vel
    velocity = velocity_grid(
        offset,
        slab_vel,
        first_count,
        second_offset,
        column_vel,
        second_count,
        velocity_factor.shape[2],
    )
    vel_first = moments(velocity_factor, velocity[..., None] * velocity_factor[None], vel_cells)
    next_plane = from_behind(velocity_factor, "vert", -1)
    next_column = from_behind(velocity_factor, GX, -1)
    following = jnp.concatenate([velocity_factor[1:], next_plane], axis=0)
    beside = jnp.concatenate([velocity_factor[:, 1:], next_column], axis=1)
    pair_sums = jnp.stack(
        [
            jnp.einsum("xyzr,xyzs->rs", velocity_factor, following, precision=HIGHEST),
            jnp.einsum("xyzr,xyzs->rs", velocity_factor, beside, precision=HIGHEST),
            jnp.einsum(
                "xyzr,xyzs->rs",
                velocity_factor[:, :, :-1],
                velocity_factor[:, :, 1:],
                precision=HIGHEST,
            ),
        ]
    )
    vel_second = 0.5 * (pair_sums - jnp.swapaxes(pair_sums, 1, 2)) / vel_cells
    vel_packed = (vel_first + vel_second).reshape(-1)
    vel_mats = split_parts(
        staged_total(vel_packed, (("gx_1", "gx_2"), ("gx_0", "vert"))).reshape(vel_first.shape)
    )

    def position_rate(values):
        return apply_pair(
            position_slopes(values), vel_mats[0], gravity[..., None] * values[None], vel_mats[1]
        )

    initial = jnp.einsum("xyzs,sr->xyzr", position_factor, coefficients, precision=HIGHEST)
    section_one = initial + TIME_STEP * position_rate(initial)
    section_two = 0.75 * initial + 0.25 * (section_one + TIME_STEP * position_rate(section_one))
    final_section = 1.0 / 3.0 * initial + 2.0 / 3.0 * (
        section_two + TIME_STEP * position_rate(section_two)
    )
    gram_part = (
        jnp.einsum("xyzr,xyzs->rs", final_section, final_section, precision=HIGHEST) / pos_cells
    )
    raw_terms = jnp.stack(
        [
            final_first_moments(final_section, pos_cells),
            moments(final_section, gravity[..., None] * final_section[None], pos_cells),
        ]
    )
    local_packed = jnp.concatenate([gram_part[None], raw_terms[0] + raw_terms[1]])
    packed = staged_total(local_packed.reshape(-1), (("gx_0", "gx_1", "gx_2"),)).reshape(
        local_packed.shape
    )
    gram_matrix = 0.5 * (packed[0] + packed[0].T)
    second_raw, first_raw = split_parts(packed[1:])
    summed_terms = jnp.stack([first_raw, second_raw])
    inv_root, root_part = newton_schulz(gram_matrix)
    new_position = jnp.einsum("xyzs,sr->xyzr", final_section, inv_root, precision=HIGHEST)
    pos_mats = jnp.einsum("ir,ndij,js->ndrs", inv_root, summed_terms, inv_root, precision=HIGHEST)
    coupled_core = root_part + TIME_STEP * (
        sandwich(pos_mats[0], root_part, vel_mats[0])
        + sandwich(pos_mats[1], root_part, vel_mats[1])
    )

    def velocity_rate(values):
        return apply_pair(
            velocity[..., None] * values[None], pos_mats[0], velocity_slopes(values), pos_mats[1]
        )

    vel_initial = jnp.einsum("abcs,rs->abcr", velocity_factor, coupled_core, precision=HIGHEST)
    vel_section = vel_initial + TIME_STEP * velocity_rate(vel_initial)
    new_velocity = 0.5 * vel_initial + 0.5 * (vel_section + TIME_STEP * velocity_rate(vel_section))
    return (new_position, new_velocity)


def solution(mesh):
    finer = Mesh(
        mesh.devices.reshape(8, 4, 2, mesh.shape["vert"]), ("gx_0", "gx_1", "gx_2", "vert")
    )
    in_specs = (P(GX, None, None, None), P(), P("vert", GX, None, None), P(None, GX, None, None))
    out_specs = (P(GX, None, None, None), P("vert", GX, None, None))
    return jax.shard_map(
        per_device, mesh=finer, in_specs=in_specs, out_specs=out_specs, check_vma=False
    )
```
